256 devices in a mesh: grp: 8 (over y_hi, x), blk: 32 (over y_lo, z, core).
Axes of the slice: x: 4, y: 4 (y_hi: 2, y_lo: 2; y = y_hi * 2 + y_lo), z: 8, core: 2. Of those that a mesh axis runs over, the one named last changes fastest.
Arguments:
- features: bfloat16 [65536, 1536], P(('grp', 'blk')), may hold values from -2 to 2
- queries: bfloat16 [65536, 768], P(('grp', 'blk')), may hold values from -6 to 6
- key_vectors: bfloat16 [65536, 768], P(('grp', 'blk')), may hold values from -6 to 6
- values: bfloat16 [65536, 768], P(('grp', 'blk')), may hold values from -8 to 8
- record_lengths: int32 [128], replicated, may hold values from 1 to 1024, 65536 in all
- output_weight: bfloat16 [768, 1536], replicated, may hold values from -0.21875 to 0.21875
- norm_gain: float32 [1536], replicated, may hold values from 0.5 to 2
- norm_bias: float32 [1536], replicated, may hold values from -3 to 3
- depthwise_taps: float32 [31, 1536], replicated, may hold values from -1 to 1
- conv_gain: float32 [1536], replicated, may hold values from 0.5 to 2
- conv_bias: float32 [1536], replicated, may hold values from -3 to 3
- pointwise_weight: bfloat16 [1536, 1536], replicated, may hold values from -0.15625 to 0.15625
Outputs:
- block_out: bfloat16 [65536, 1536], P(('grp', 'blk'))
The draws below stay inside these ranges and needn't reach their ends.
Inputs may be any that keep to these rules, and one draw needn't show every extreme that they name: `record_lengths`: recording lengths in frames, summing to 65536; the longest is exactly 1024.
All inputs are finite; a program needn't handle non-finite values.
Results may differ from the reference program's by a relative error of at most 0.013.
Values may be sent and summed in bfloat16 or wider, within the bound.
No kernel may reach another device: no remote copies, remote signals or barrier semaphores. Data moves between devices by JAX's collectives and lax.ppermute only.
A program may use at most 128 MiB of HBM per device.

```python
import math
import jax
import jax.numpy as jnp
import numpy as np
from jax import lax

D = 1536
HEADS = 12
HD = 64
KTAPS = 31
FR = 256
REACH = 4
MAXLEN = 1024
TOTAL = 65536
NREC = 128


def query_key_pair(key):
    query_key = jax.random.fold_in(key, 11)
    keys_key = jax.random.fold_in(key, 12)
    shape = (TOTAL, HEADS * HD)
    query_out = jnp.clip(jax.random.normal(query_key, shape, jnp.float32), -4.0, 4.0)
    keys_out = jnp.clip(jax.random.normal(keys_key, shape, jnp.float32), -4.0, 4.0)
    return (query_out, keys_out)


def draw_queries(key, part):
    return query_key_pair(key)[0].astype(jnp.bfloat16)


def draw_key_vectors(key, part):
    return query_key_pair(key)[1].astype(jnp.bfloat16)


def draw_features(key, part):
    base_key = jax.random.fold_in(key, 21)
    column_key = jax.random.fold_in(key, 22)
    row_key = jax.random.fold_in(key, 23)
    columns = jnp.exp(jax.random.uniform(column_key, (D,), jnp.float32, math.log(0.1), math.log(1.0)))
    row_scales = jnp.exp(jax.random.uniform(row_key, (TOTAL,), jnp.float32, math.log(0.05), math.log(0.5)))
    base = jnp.clip(jax.random.normal(base_key, (TOTAL, D), jnp.float32), -4.0, 4.0)
    return (base * row_scales[:, None] * columns[None, :]).astype(jnp.bfloat16)


def levels(own_key, dims, cuts, smallest, high):
    def one(axis_at, shards_of):
        heights = jax.random.uniform(jax.random.fold_in(jax.random.fold_in(own_key, 6), axis_at), (shards_of,), jnp.float32, smallest / len(cuts), high / len(cuts))
        return jnp.repeat(jnp.exp(heights), dims[axis_at] // shards_of).reshape((-1,) + (1,) * (len(dims) - axis_at - 1))

    level = one(*cuts[0])
    for cut in cuts[1:]:
        level = level * one(*cut)
    return level


def split_up(number_of, total, most, slope):
    weights = [(1 << 20) // math.isqrt(grade ** slope) + 1 for grade in range(2, number_of + 1)]
    spare, given = total - most - (number_of - 1), [1] * (number_of - 1)
    while spare > 0:
        free = [i for i in range(number_of - 1) if given[i] < most]
        whole, left = sum([weights[i] for i in free]), spare
        for i in free:
            more = min(most - given[i], max(1, left * weights[i] // whole), spare)
            given[i] = given[i] + more
            spare = spare - more
    return np.array([most] + given)


def ragged(key, number_of, total, most, skew):
    if number_of == 2:
        one = jax.random.randint(key, (), max(1, total - most), min(most, total - 1) + 1)
        return jnp.stack([one, total - one])
    tallies = jnp.asarray(split_up(number_of, total, most, skew), jnp.int32)
    pairs = (number_of - 1) // 2
    source_of, sink = tallies[1:1 + 2 * pairs:2], tallies[2:2 + 2 * pairs:2]
    slack = jnp.minimum(source_of - 1, most - sink)
    moved = jax.random.randint(jax.random.fold_in(key, 1), (pairs,), 0, 1 << 20) % (slack + 1)
    tallies = tallies.at[1:1 + 2 * pairs:2].set(source_of - moved).at[2:2 + 2 * pairs:2].set(sink + moved)
    return tallies[jax.random.permutation(jax.random.fold_in(key, 2), number_of)]


def bell_draw(stream_key, dims, deviation, reach, split=(), kind=jnp.bfloat16):
    array = deviation * jax.random.normal(stream_key, dims, jnp.float32)
    if split:
        array = array * levels(stream_key, dims, split, -0.22, 0.18)
    return jnp.clip(array, -reach, reach).astype(kind)


def setup_inputs(seed: int = 0) -> dict:
    arg_keys = jax.random.split(jax.random.key(seed), 13)
    features = draw_features(jax.random.fold_in(arg_keys[12], 71), 0)
    queries = draw_queries(jax.random.fold_in(arg_keys[12], 71), 0)
    key_vectors = draw_key_vectors(jax.random.fold_in(arg_keys[12], 71), 0)
    values = bell_draw(arg_keys[3], (TOTAL, HEADS * HD), 2.0, 8.0, ((0, 256),))
    record_lengths = ragged(arg_keys[4], NREC, TOTAL, MAXLEN, 2).astype(jnp.int32)
    output_weight = bell_draw(arg_keys[5], (HEADS * HD, D), (HEADS * HD) ** -0.5, 0.21875)
    norm_gain = jnp.clip(jnp.exp(jax.random.uniform(arg_keys[6], (D,), jnp.float32, math.log(0.5), math.log(2.0))), 0.5, 2.0)
    norm_bias = bell_draw(arg_keys[7], (D,), 0.5, 3.0, (), jnp.float32)
    depthwise_taps = bell_draw(arg_keys[8], (KTAPS, D), KTAPS ** -0.5, 1.0, (), jnp.float32)
    conv_gain = jnp.clip(jnp.exp(jax.random.uniform(arg_keys[9], (D,), jnp.float32, math.log(0.5), math.log(2.0))), 0.5, 2.0)
    conv_bias = bell_draw(arg_keys[10], (D,), 0.5, 3.0, (), jnp.float32)
    pointwise_weight = bell_draw(arg_keys[11], (D, D), D ** -0.5, 0.15625)
    return dict(features=features, queries=queries, key_vectors=key_vectors, values=values, record_lengths=record_lengths, output_weight=output_weight, norm_gain=norm_gain, norm_bias=norm_bias, depthwise_taps=depthwise_taps, conv_gain=conv_gain, conv_bias=conv_bias, pointwise_weight=pointwise_weight)


def segment_of(positions, starts):
    return lax.optimization_barrier(jnp.sum((starts[None, :] <= positions[:, None]).astype(jnp.int32), axis=1)) - 1

def reference(features, queries, key_vectors, values, record_lengths, output_weight, norm_gain, norm_bias, depthwise_taps, conv_gain, conv_bias, pointwise_weight):
    nblocks = TOTAL // FR
    rec_ends = jnp.cumsum(record_lengths).astype(jnp.int32)
    starts = (rec_ends - record_lengths).astype(jnp.int32)
    positions = jnp.arange(TOTAL, dtype=jnp.int32)
    recs = segment_of(positions, starts).astype(jnp.int32)
    margin = REACH * FR
    window = (2 * REACH + 1) * FR
    fill = -jnp.ones((margin,), jnp.int32)
    rec_padded = jnp.concatenate([fill, recs, fill]).astype(jnp.int32)
    key_padded = jnp.pad(key_vectors, ((margin, margin), (0, 0)))
    value_padded = jnp.pad(values, ((margin, margin), (0, 0)))
    scale = HD ** (-0.5)

    def attend_block(block):
        first = (block * FR).astype(jnp.int32)
        query = lax.dynamic_slice_in_dim(queries, first, FR, 0).astype(jnp.float32).reshape(FR, HEADS, HD)
        keyset = lax.dynamic_slice_in_dim(key_padded, first, window, 0).astype(jnp.float32).reshape(window, HEADS, HD)
        valset = lax.dynamic_slice_in_dim(value_padded, first, window, 0).astype(jnp.float32).reshape(window, HEADS, HD)
        rec_query = lax.dynamic_slice_in_dim(recs, first, FR, 0)
        rec_key = lax.dynamic_slice_in_dim(rec_padded, first, window, 0)
        same_rec = (rec_query[:, None] == rec_key[None, :])[None]
        scores = jnp.einsum('qhd,khd->hqk', query, keyset) * scale
        scores = jnp.where(same_rec, scores, -1e+30)
        maxima = lax.optimization_barrier(jnp.max(scores, axis=-1, keepdims=True))
        expw = jnp.where(same_rec, jnp.exp(scores - maxima), 0.0)
        totals = lax.optimization_barrier(jnp.sum(expw, axis=-1))
        rounded = lax.optimization_barrier(expw.astype(jnp.bfloat16)).astype(jnp.float32)
        summed = jnp.einsum('hqk,khd->qhd', rounded, valset)
        return (summed / jnp.transpose(totals)[:, :, None]).reshape(FR, HEADS * HD).astype(jnp.bfloat16)
    attended = lax.map(attend_block, jnp.arange(nblocks, dtype=jnp.int32)).reshape(TOTAL, HEADS * HD)
    projected = jnp.dot(attended, output_weight, preferred_element_type=jnp.float32)
    resid = lax.optimization_barrier((features.astype(jnp.float32) + projected).astype(jnp.bfloat16))
    resid32 = resid.astype(jnp.float32)
    center = lax.optimization_barrier(jnp.mean(resid32, axis=1, keepdims=True))
    spread = lax.optimization_barrier(jnp.mean((resid32 - center) ** 2, axis=1, keepdims=True))
    normed = ((resid32 - center) * lax.rsqrt(spread + 1e-05) * norm_gain + norm_bias).astype(jnp.bfloat16)
    normed = lax.optimization_barrier(normed)
    rim_width = (KTAPS - 1) // 2
    normed_padded = jnp.pad(normed, ((rim_width, rim_width), (0, 0)))
    rim_fill = -jnp.ones((rim_width,), jnp.int32)
    rec_conv = jnp.concatenate([rim_fill, recs, rim_fill]).astype(jnp.int32)

    def conv_block(block):
        first = (block * FR).astype(jnp.int32)
        frames = lax.dynamic_slice_in_dim(normed_padded, first, FR + 2 * rim_width, 0).astype(jnp.float32)
        rec_frames = lax.dynamic_slice_in_dim(rec_conv, first, FR + 2 * rim_width, 0)
        rec_query = lax.dynamic_slice_in_dim(recs, first, FR, 0)
        summed = jnp.zeros((FR, D), jnp.float32)
        for tap in range(KTAPS):
            same_rec = (rec_frames[tap:tap + FR] == rec_query)[:, None]
            summed = summed + jnp.where(same_rec, frames[tap:tap + FR] * depthwise_taps[tap], 0.0)
        shifted = summed * conv_gain + conv_bias
        return (shifted * jax.nn.sigmoid(shifted)).astype(jnp.bfloat16)
    act = lax.map(conv_block, jnp.arange(nblocks, dtype=jnp.int32)).reshape(TOTAL, D)
    return (resid32 + jnp.dot(act, pointwise_weight, preferred_element_type=jnp.float32)).astype(jnp.bfloat16)
```

```python
import jax
import jax.numpy as jnp
from jax import lax
from jax.sharding import PartitionSpec as P
from jax.experimental import pallas as pl
from jax.experimental.pallas import tpu as pltpu

HEADS = 12
HD = 64
REACH = 4


def shifted_2(block, axis, distance):
    devices = range(lax.axis_size(axis))
    route = [(i - distance, i) for i in devices if i - distance in devices]
    return lax.ppermute(block, axis, route)


def padded(block, sides, width):
    for axis, dim in sides:
        count = lax.axis_size(axis)
        forward = [(i, i + 1) for i in range(count - 1)]
        backward = [(target, source) for source, target in forward]
        low = lax.ppermute(
            lax.slice_in_dim(block, block.shape[dim] - width, None, axis=dim), axis, forward
        )
        high = lax.ppermute(lax.slice_in_dim(block, 0, width, axis=dim), axis, backward)
        block = jnp.concatenate([low, block, high], axis=dim)
    return block


def segment_of(positions, starts):
    return jnp.sum((starts[None, :] <= positions[:, None]).astype(jnp.int32), axis=1) - 1


def from_before(moving):
    return shifted_2(moving, ("grp", "blk"), 1)


def from_after(moving):
    return shifted_2(moving, ("grp", "blk"), -1)


NBLK = 2 * REACH + 1


def attend_kernel(recq_ref, reck_ref, q_ref, *refs):
    k_refs = refs[:NBLK]
    v_refs = refs[NBLK : 2 * NBLK]
    out_ref = refs[2 * NBLK]
    s_scr = refs[2 * NBLK + 1]
    rec_q = recq_ref[...]
    for hh in range(2):
        cols = slice(hh * HD, (hh + 1) * HD)
        q_h = q_ref[:, cols]
        top = None
        for j in range(NBLK):
            s = lax.dot_general(
                q_h, k_refs[j][:, cols], (((1,), (1,)), ((), ())),
                preferred_element_type=jnp.float32,
            ) * (HD ** (-0.5))
            s = jnp.where(rec_q == reck_ref[j : j + 1, :], s, -1e30)
            s_scr[j] = s
            row = jnp.max(s, axis=1, keepdims=True)
            top = row if top is None else jnp.maximum(top, row)
        total = None
        acc = None
        for j in range(NBLK):
            p = jnp.exp(s_scr[j] - top)
            part = jnp.sum(p, axis=1, keepdims=True)
            prod = jnp.dot(p.astype(jnp.bfloat16), v_refs[j][:, cols],
                           preferred_element_type=jnp.float32)
            total = part if total is None else total + part
            acc = prod if acc is None else acc + prod
        out_ref[:, cols] = (acc / total).astype(out_ref.dtype)


def attend(rec_q, rec_k, query, keys, vals):
    frames, width = query.shape
    pair = 2 * HD
    tile = pl.BlockSpec((frames, pair), lambda g: (0, g))
    return pl.pallas_call(
        attend_kernel,
        grid=(width // pair,),
        in_specs=[
            pl.BlockSpec(rec_q.shape, lambda g: (0, 0)),
            pl.BlockSpec(rec_k.shape, lambda g: (0, 0)),
            tile,
        ]
        + [tile] * (2 * NBLK),
        out_specs=tile,
        out_shape=jax.ShapeDtypeStruct((frames, width), jnp.bfloat16),
        scratch_shapes=[pltpu.VMEM((NBLK, frames, frames), jnp.float32)],
    )(rec_q, rec_k, query, *keys, *vals)


def shards(
    features,
    queries,
    key_vectors,
    values,
    record_lengths,
    output_weight,
    norm_gain,
    norm_bias,
    depthwise_taps,
    conv_gain,
    conv_bias,
    pointwise_weight,
):
    frames = features.shape[0]
    per_group = lax.axis_size("blk")
    nblocks = lax.axis_size("grp") * per_group
    block_here = lax.axis_index("grp") * per_group + lax.axis_index("blk")
    rec_ends = jnp.cumsum(record_lengths)
    starts = rec_ends - record_lengths
    offsets = jnp.arange(frames, dtype=jnp.int32)
    own_rec = segment_of(block_here * frames + offsets, starts)

    key_blocks = block_here + jnp.arange(-REACH, REACH + 1, dtype=jnp.int32)
    key_pos = (key_blocks[:, None] * frames + offsets[None, :]).reshape(-1)
    key_inside = ((key_blocks >= 0) & (key_blocks < nblocks))[:, None]
    key_rec = jnp.where(key_inside, segment_of(key_pos, starts).reshape(NBLK, frames), -1)
    rows = -(-NBLK // 8) * 8
    key_rec = jnp.pad(key_rec, ((0, rows - NBLK), (0, 0)), constant_values=-1)

    before_k, before_v, after_k, after_v = [], [], [], []
    moving = (key_vectors, values)
    for distance in range(1, REACH + 1):
        moving = from_before(moving)
        before_k.append(moving[0])
        before_v.append(moving[1])
    moving = (key_vectors, values)
    for distance in range(1, REACH + 1):
        moving = from_after(moving)
        after_k.append(moving[0])
        after_v.append(moving[1])
    keys = before_k[::-1] + [key_vectors] + after_k
    vals = before_v[::-1] + [values] + after_v
    attended = attend(own_rec[:, None], key_rec, queries, keys, vals)
    projected = jnp.dot(attended, output_weight, preferred_element_type=jnp.float32)
    resid = lax.optimization_barrier(
        (features.astype(jnp.float32) + projected).astype(jnp.bfloat16)
    )
    resid32 = resid.astype(jnp.float32)
    center = jnp.mean(resid32, axis=1, keepdims=True)
    spread = jnp.mean((resid32 - center) ** 2, axis=1, keepdims=True)
    normed = ((resid32 - center) * lax.rsqrt(spread + 1e-05) * norm_gain + norm_bias).astype(
        jnp.bfloat16
    )
    rim_width = (depthwise_taps.shape[0] - 1) // 2
    extended = padded(normed, ((("grp", "blk"), 0),), rim_width)
    ext_positions = (
        block_here * frames - rim_width + jnp.arange(frames + 2 * rim_width, dtype=jnp.int32)
    )
    ext_inside = (ext_positions >= 0) & (ext_positions < nblocks * frames)
    ext_rec = jnp.where(ext_inside, segment_of(ext_positions, starts), -1)
    extended32 = lax.optimization_barrier(extended).astype(jnp.float32)
    summed = jnp.zeros((frames, normed.shape[1]), jnp.float32)
    for tap in range(depthwise_taps.shape[0]):
        same_rec = (ext_rec[tap : tap + frames] == own_rec)[:, None]
        summed = summed + jnp.where(
            same_rec, extended32[tap : tap + frames] * depthwise_taps[tap], 0.0
        )
    shifted = summed * conv_gain + conv_bias
    act = (shifted * jax.nn.sigmoid(shifted)).astype(jnp.bfloat16)
    return (resid32 + jnp.dot(act, pointwise_weight, preferred_element_type=jnp.float32)).astype(
        jnp.bfloat16
    )


def solution(mesh):
    in_specs = (
        P(("grp", "blk"), None),
        P(("grp", "blk"), None),
        P(("grp", "blk"), None),
        P(("grp", "blk"), None),
        P(),
        P(),
        P(),
        P(),
        P(),
        P(),
        P(),
        P(),
    )
    out_specs = P(("grp", "blk"), None)
    return jax.shard_map(shards, mesh=mesh, in_specs=in_specs, out_specs=out_specs, check_vma=False)
```

```python
import jax
import jax.numpy as jnp
from jax import lax
from jax.sharding import PartitionSpec as P
from jax.experimental import pallas as pl
from jax.experimental.pallas import tpu as pltpu

HEADS = 12
HD = 64
REACH = 4


def shifted_2(block, axis, distance):
    devices = range(lax.axis_size(axis))
    route = [(i - distance, i) for i in devices if i - distance in devices]
    return lax.ppermute(block, axis, route)


def padded(block, sides, width):
    for axis, dim in sides:
        count = lax.axis_size(axis)
        forward = [(i, i + 1) for i in range(count - 1)]
        backward = [(target, source) for source, target in forward]
        low = lax.ppermute(
            lax.slice_in_dim(block, block.shape[dim] - width, None, axis=dim), axis, forward
        )
        high = lax.ppermute(lax.slice_in_dim(block, 0, width, axis=dim), axis, backward)
        block = jnp.concatenate([low, block, high], axis=dim)
    return block


def segment_of(positions, starts):
    return jnp.sum((starts[None, :] <= positions[:, None]).astype(jnp.int32), axis=1) - 1


def from_before(moving):
    return shifted_2(moving, ("grp", "blk"), 1)


def from_after(moving):
    return shifted_2(moving, ("grp", "blk"), -1)


NBLK = 2 * REACH + 1


def attend_kernel(flags_ref, recq_ref, reck_ref, q_ref, *refs):
    k_refs = refs[:NBLK]
    v_refs = refs[NBLK : 2 * NBLK]
    out_ref = refs[2 * NBLK]
    s_scr, m_scr, l_scr, acc_scr = refs[2 * NBLK + 1 :]
    rec_q = recq_ref[...]
    others = [j for j in range(NBLK) if j != REACH]
    for hh in range(2):
        cols = slice(hh * HD, (hh + 1) * HD)
        q_h = q_ref[:, cols]

        def scores(j):
            s = lax.dot_general(
                q_h, k_refs[j][:, cols], (((1,), (1,)), ((), ())),
                preferred_element_type=jnp.float32,
            ) * (HD ** (-0.5))
            return jnp.where(rec_q == reck_ref[j : j + 1, :], s, -1e30)

        s = scores(REACH)
        s_scr[REACH] = s
        m_scr[...] = jnp.max(s, axis=1, keepdims=True)
        for j in others:
            @pl.when(flags_ref[j] != 0)
            def _(j=j):
                s = scores(j)
                s_scr[j] = s
                m_scr[...] = jnp.maximum(m_scr[...], jnp.max(s, axis=1, keepdims=True))

        top = m_scr[...]

        def weigh(j):
            p = jnp.exp(s_scr[j] - top)
            part = jnp.sum(p, axis=1, keepdims=True)
            prod = jnp.dot(p.astype(jnp.bfloat16), v_refs[j][:, cols],
                           preferred_element_type=jnp.float32)
            return part, prod

        part, prod = weigh(REACH)
        l_scr[...] = part
        acc_scr[...] = prod
        for j in others:
            @pl.when(flags_ref[j] != 0)
            def _(j=j):
                part, prod = weigh(j)
                l_scr[...] += part
                acc_scr[...] += prod

        out_ref[:, cols] = (acc_scr[...] / l_scr[...]).astype(out_ref.dtype)


def attend(flags, rec_q, rec_k, query, kvs):
    frames, width = query.shape
    pair = 2 * HD
    steps = width // pair
    q_tile = pl.BlockSpec((frames, pair), lambda g, f: (0, g))
    k_tile = pl.BlockSpec((frames, pair), lambda g, f: (0, g))
    v_tile = pl.BlockSpec((frames, pair), lambda g, f: (0, g + steps))
    grid_spec = pltpu.PrefetchScalarGridSpec(
        num_scalar_prefetch=1,
        grid=(steps,),
        in_specs=[
            pl.BlockSpec(rec_q.shape, lambda g, f: (0, 0)),
            pl.BlockSpec(rec_k.shape, lambda g, f: (0, 0)),
            q_tile,
        ]
        + [k_tile] * NBLK
        + [v_tile] * NBLK,
        out_specs=q_tile,
        scratch_shapes=[
            pltpu.VMEM((NBLK, frames, frames), jnp.float32),
            pltpu.VMEM((frames, 1), jnp.float32),
            pltpu.VMEM((frames, 1), jnp.float32),
            pltpu.VMEM((frames, HD), jnp.float32),
        ],
    )
    return pl.pallas_call(
        attend_kernel,
        grid_spec=grid_spec,
        out_shape=jax.ShapeDtypeStruct((frames, width), jnp.bfloat16),
    )(flags, rec_q, rec_k, query, *kvs, *kvs)


CT = 128
RT = 128


def conv_kernel(extrec_ref, ownrec_ref, ext_ref, taps_ref, gain_ref, bias_ref, out_ref, x_scr):
    x_scr[...] = ext_ref[...].astype(jnp.float32)
    frames = out_ref.shape[0]
    ntaps = taps_ref.shape[0]
    for r0 in range(0, frames, RT):
        own = ownrec_ref[r0 : r0 + RT, :]
        acc = jnp.zeros((RT, out_ref.shape[1]), jnp.float32)
        for j in range(ntaps):
            same = extrec_ref[r0 + j : r0 + j + RT, :] == own
            acc = acc + jnp.where(same, x_scr[r0 + j : r0 + j + RT, :] * taps_ref[j : j + 1, :], 0.0)
        y = acc * gain_ref[...] + bias_ref[...]
        out_ref[r0 : r0 + RT, :] = (y / (1.0 + jnp.exp(-y))).astype(out_ref.dtype)


def depthwise(ext_rec, own_rec, ext, taps, gain, bias):
    rows, width = ext.shape
    frames = own_rec.shape[0]
    ntaps = taps.shape[0]
    col = lambda c: (0, c)
    return pl.pallas_call(
        conv_kernel,
        grid=(width // CT,),
        in_specs=[
            pl.BlockSpec(ext_rec.shape, lambda c: (0, 0)),
            pl.BlockSpec(own_rec.shape, lambda c: (0, 0)),
            pl.BlockSpec((rows, CT), col),
            pl.BlockSpec((ntaps, CT), col),
            pl.BlockSpec((1, CT), col),
            pl.BlockSpec((1, CT), col),
        ],
        out_specs=pl.BlockSpec((frames, CT), col),
        out_shape=jax.ShapeDtypeStruct((frames, width), jnp.bfloat16),
        scratch_shapes=[pltpu.VMEM((rows, CT), jnp.float32)],
    )(ext_rec, own_rec, ext, taps, gain, bias)


def shards(
    features,
    queries,
    key_vectors,
    values,
    record_lengths,
    output_weight,
    norm_gain,
    norm_bias,
    depthwise_taps,
    conv_gain,
    conv_bias,
    pointwise_weight,
):
    frames = features.shape[0]
    per_group = lax.axis_size("blk")
    nblocks = lax.axis_size("grp") * per_group
    block_here = lax.axis_index("grp") * per_group + lax.axis_index("blk")
    rec_ends = jnp.cumsum(record_lengths)
    starts = rec_ends - record_lengths
    offsets = jnp.arange(frames, dtype=jnp.int32)
    own_rec = segment_of(block_here * frames + offsets, starts)

    key_blocks = block_here + jnp.arange(-REACH, REACH + 1, dtype=jnp.int32)
    key_pos = (key_blocks[:, None] * frames + offsets[None, :]).reshape(-1)
    key_inside = ((key_blocks >= 0) & (key_blocks < nblocks))[:, None]
    key_rec = jnp.where(key_inside, segment_of(key_pos, starts).reshape(NBLK, frames), -1)
    rows = -(-NBLK // 8) * 8
    key_rec = jnp.pad(key_rec, ((0, rows - NBLK), (0, 0)), constant_values=-1)

    own_kv = jnp.concatenate([key_vectors, values], axis=1)
    before, after = [], []
    moving = own_kv
    for distance in range(1, REACH + 1):
        moving = from_before(moving)
        before.append(moving)
    moving = own_kv
    for distance in range(1, REACH + 1):
        moving = from_after(moving)
        after.append(moving)
    kvs = before[::-1] + [own_kv] + after
    first_rec = key_rec[:NBLK, 0]
    last_rec = key_rec[:NBLK, frames - 1]
    flags = (key_inside[:, 0] & (first_rec <= own_rec[frames - 1]) & (last_rec >= own_rec[0]))
    attended = attend(flags.astype(jnp.int32), own_rec[:, None], key_rec, queries, kvs)
    projected = jnp.dot(attended, output_weight, preferred_element_type=jnp.float32)
    resid = lax.optimization_barrier(
        (features.astype(jnp.float32) + projected).astype(jnp.bfloat16)
    )
    resid32 = resid.astype(jnp.float32)
    center = jnp.mean(resid32, axis=1, keepdims=True)
    spread = jnp.mean((resid32 - center) ** 2, axis=1, keepdims=True)
    normed = ((resid32 - center) * lax.rsqrt(spread + 1e-05) * norm_gain + norm_bias).astype(
        jnp.bfloat16
    )
    rim_width = (depthwise_taps.shape[0] - 1) // 2
    extended = padded(normed, ((("grp", "blk"), 0),), rim_width)
    ext_positions = (
        block_here * frames - rim_width + jnp.arange(frames + 2 * rim_width, dtype=jnp.int32)
    )
    ext_inside = (ext_positions >= 0) & (ext_positions < nblocks * frames)
    ext_rec = jnp.where(ext_inside, segment_of(ext_positions, starts), -1)
    rows = -(-(frames + 2 * rim_width) // 16) * 16
    ext = jnp.pad(extended, ((0, rows - extended.shape[0]), (0, 0)))
    ext_rec = jnp.pad(ext_rec, (0, rows - ext_rec.shape[0]), constant_values=-1)
    act = depthwise(
        ext_rec[:, None], own_rec[:, None], ext, depthwise_taps,
        conv_gain[None, :], conv_bias[None, :],
    )
    return (resid32 + jnp.dot(act, pointwise_weight, preferred_element_type=jnp.float32)).astype(
        jnp.bfloat16
    )


def solution(mesh):
    in_specs = (
        P(("grp", "blk"), None),
        P(("grp", "blk"), None),
        P(("grp", "blk"), None),
        P(("grp", "blk"), None),
        P(),
        P(),
        P(),
        P(),
        P(),
        P(),
        P(),
        P(),
    )
    out_specs = P(("grp", "blk"), None)
    return jax.shard_map(shards, mesh=mesh, in_specs=in_specs, out_specs=out_specs, check_vma=False)
```

```python
import jax
import jax.numpy as jnp
from jax import lax
from jax.sharding import PartitionSpec as P
from jax.experimental import pallas as pl
from jax.experimental.pallas import tpu as pltpu

HEADS = 12
HD = 64
REACH = 4


def shifted_2(block, axis, distance):
    devices = range(lax.axis_size(axis))
    route = [(i - distance, i) for i in devices if i - distance in devices]
    return lax.ppermute(block, axis, route)


def padded(block, sides, width):
    for axis, dim in sides:
        count = lax.axis_size(axis)
        forward = [(i, i + 1) for i in range(count - 1)]
        backward = [(target, source) for source, target in forward]
        low = lax.ppermute(
            lax.slice_in_dim(block, block.shape[dim] - width, None, axis=dim), axis, forward
        )
        high = lax.ppermute(lax.slice_in_dim(block, 0, width, axis=dim), axis, backward)
        block = jnp.concatenate([low, block, high], axis=dim)
    return block


def segment_of(positions, starts):
    return jnp.sum((starts[None, :] <= positions[:, None]).astype(jnp.int32), axis=1) - 1


def from_before(moving):
    return shifted_2(moving, ("grp", "blk"), 1)


def from_after(moving):
    return shifted_2(moving, ("grp", "blk"), -1)


NBLK = 2 * REACH + 1


def attend_kernel(recq_ref, reck_ref, q_ref, *refs):
    k_refs = refs[:NBLK]
    v_refs = refs[NBLK : 2 * NBLK]
    out_ref = refs[2 * NBLK]
    s_scr = refs[2 * NBLK + 1]
    rec_q = recq_ref[...]
    for hh in range(2):
        cols = slice(hh * HD, (hh + 1) * HD)
        q_h = q_ref[:, cols]
        top = None
        for j in range(NBLK):
            s = lax.dot_general(
                q_h, k_refs[j][:, cols], (((1,), (1,)), ((), ())),
                preferred_element_type=jnp.float32,
            ) * (HD ** (-0.5))
            s = jnp.where(rec_q == reck_ref[j : j + 1, :], s, -1e30)
            s_scr[j] = s
            row = jnp.max(s, axis=1, keepdims=True)
            top = row if top is None else jnp.maximum(top, row)
        total = None
        acc = None
        for j in range(NBLK):
            p = jnp.exp(s_scr[j] - top)
            part = jnp.sum(p, axis=1, keepdims=True)
            prod = jnp.dot(p.astype(jnp.bfloat16), v_refs[j][:, cols],
                           preferred_element_type=jnp.float32)
            total = part if total is None else total + part
            acc = prod if acc is None else acc + prod
        out_ref[:, cols] = (acc / total).astype(out_ref.dtype)


def attend(rec_q, rec_k, query, keys, vals):
    frames, width = query.shape
    pair = 2 * HD
    tile = pl.BlockSpec((frames, pair), lambda g: (0, g))
    return pl.pallas_call(
        attend_kernel,
        grid=(width // pair,),
        in_specs=[
            pl.BlockSpec(rec_q.shape, lambda g: (0, 0)),
            pl.BlockSpec(rec_k.shape, lambda g: (0, 0)),
            tile,
        ]
        + [tile] * (2 * NBLK),
        out_specs=tile,
        out_shape=jax.ShapeDtypeStruct((frames, width), jnp.bfloat16),
        scratch_shapes=[pltpu.VMEM((NBLK, frames, frames), jnp.float32)],
    )(rec_q, rec_k, query, *keys, *vals)


def shards(
    features,
    queries,
    key_vectors,
    values,
    record_lengths,
    output_weight,
    norm_gain,
    norm_bias,
    depthwise_taps,
    conv_gain,
    conv_bias,
    pointwise_weight,
):
    frames = features.shape[0]
    per_group = lax.axis_size("blk")
    nblocks = lax.axis_size("grp") * per_group
    block_here = lax.axis_index("grp") * per_group + lax.axis_index("blk")
    rec_ends = jnp.cumsum(record_lengths)
    starts = rec_ends - record_lengths
    offsets = jnp.arange(frames, dtype=jnp.int32)
    own_rec = segment_of(block_here * frames + offsets, starts)

    key_blocks = block_here + jnp.arange(-REACH, REACH + 1, dtype=jnp.int32)
    key_pos = (key_blocks[:, None] * frames + offsets[None, :]).reshape(-1)
    key_inside = ((key_blocks >= 0) & (key_blocks < nblocks))[:, None]
    key_rec = jnp.where(key_inside, segment_of(key_pos, starts).reshape(NBLK, frames), -1)
    rows = -(-NBLK // 8) * 8
    key_rec = jnp.pad(key_rec, ((0, rows - NBLK), (0, 0)), constant_values=-1)

    before_k, before_v, after_k, after_v = [], [], [], []
    moving = (key_vectors, values)
    for distance in range(1, REACH + 1):
        moving = from_before(moving)
        before_k.append(moving[0])
        before_v.append(moving[1])
    moving = (key_vectors, values)
    for distance in range(1, REACH + 1):
        moving = from_after(moving)
        after_k.append(moving[0])
        after_v.append(moving[1])
    keys = before_k[::-1] + [key_vectors] + after_k
    vals = before_v[::-1] + [values] + after_v
    attended = attend(own_rec[:, None], key_rec, queries, keys, vals)
    projected = jnp.dot(attended, output_weight, preferred_element_type=jnp.float32)
    resid = lax.optimization_barrier(
        (features.astype(jnp.float32) + projected).astype(jnp.bfloat16)
    )
    resid32 = resid.astype(jnp.float32)
    center = jnp.mean(resid32, axis=1, keepdims=True)
    spread = jnp.mean((resid32 - center) ** 2, axis=1, keepdims=True)
    normed = ((resid32 - center) * lax.rsqrt(spread + 1e-05) * norm_gain + norm_bias).astype(
        jnp.bfloat16
    )
    rim_width = (depthwise_taps.shape[0] - 1) // 2
    extended = padded(normed, ((("grp", "blk"), 0),), rim_width)
    ext_positions = (
        block_here * frames - rim_width + jnp.arange(frames + 2 * rim_width, dtype=jnp.int32)
    )
    ext_inside = (ext_positions >= 0) & (ext_positions < nblocks * frames)
    ext_rec = jnp.where(ext_inside, segment_of(ext_positions, starts), -1)
    extended32 = lax.optimization_barrier(extended).astype(jnp.float32)
    summed = jnp.zeros((frames, normed.shape[1]), jnp.float32)
    for tap in range(depthwise_taps.shape[0]):
        same_rec = (ext_rec[tap : tap + frames] == own_rec)[:, None]
        summed = summed + jnp.where(
            same_rec, extended32[tap : tap + frames] * depthwise_taps[tap], 0.0
        )
    shifted = summed * conv_gain + conv_bias
    act = lax.optimization_barrier((shifted * jax.nn.sigmoid(shifted)).astype(jnp.bfloat16))
    return (resid32 + jnp.dot(act, pointwise_weight, preferred_element_type=jnp.float32)).astype(
        jnp.bfloat16
    )


def solution(mesh):
    in_specs = (
        P(("grp", "blk"), None),
        P(("grp", "blk"), None),
        P(("grp", "blk"), None),
        P(("grp", "blk"), None),
        P(),
        P(),
        P(),
        P(),
        P(),
        P(),
        P(),
        P(),
    )
    out_specs = P(("grp", "blk"), None)
    return jax.shard_map(shards, mesh=mesh, in_specs=in_specs, out_specs=out_specs, check_vma=False)
```

```python
import jax
import jax.numpy as jnp
from jax import lax
from jax.sharding import PartitionSpec as P
from jax.experimental import pallas as pl
from jax.experimental.pallas import tpu as pltpu

HEADS = 12
HD = 64
REACH = 4


def shifted_2(block, axis, distance):
    devices = range(lax.axis_size(axis))
    route = [(i - distance, i) for i in devices if i - distance in devices]
    return lax.ppermute(block, axis, route)


def padded(block, sides, width):
    for axis, dim in sides:
        count = lax.axis_size(axis)
        forward = [(i, i + 1) for i in range(count - 1)]
        backward = [(target, source) for source, target in forward]
        low = lax.ppermute(
            lax.slice_in_dim(block, block.shape[dim] - width, None, axis=dim), axis, forward
        )
        high = lax.ppermute(lax.slice_in_dim(block, 0, width, axis=dim), axis, backward)
        block = jnp.concatenate([low, block, high], axis=dim)
    return block


def segment_of(positions, starts):
    return jnp.sum((starts[None, :] <= positions[:, None]).astype(jnp.int32), axis=1) - 1


def from_before(moving):
    return shifted_2(moving, ("grp", "blk"), 1)


def from_after(moving):
    return shifted_2(moving, ("grp", "blk"), -1)


NBLK = 2 * REACH + 1


def attend_kernel(recq_ref, reck_ref, q_ref, *refs):
    k_refs = refs[:NBLK]
    v_refs = refs[NBLK : 2 * NBLK]
    out_ref = refs[2 * NBLK]
    s_scr = refs[2 * NBLK + 1]
    rec_q = recq_ref[...]
    for hh in range(2):
        cols = slice(hh * HD, (hh + 1) * HD)
        q_h = q_ref[:, cols]
        top = None
        for j in range(NBLK):
            s = lax.dot_general(
                q_h, k_refs[j][:, cols], (((1,), (1,)), ((), ())),
                preferred_element_type=jnp.float32,
            ) * (HD ** (-0.5))
            s = jnp.where(rec_q == reck_ref[j : j + 1, :], s, -1e30)
            s_scr[j] = s
            row = jnp.max(s, axis=1, keepdims=True)
            top = row if top is None else jnp.maximum(top, row)
        total = None
        acc = None
        for j in range(NBLK):
            p = jnp.exp(s_scr[j] - top)
            part = jnp.sum(p, axis=1, keepdims=True)
            prod = jnp.dot(p.astype(jnp.bfloat16), v_refs[j][:, cols],
                           preferred_element_type=jnp.float32)
            total = part if total is None else total + part
            acc = prod if acc is None else acc + prod
        out_ref[:, cols] = (acc / total).astype(out_ref.dtype)


def attend(rec_q, rec_k, query, keys, vals):
    frames, width = query.shape
    pair = 2 * HD
    tile = pl.BlockSpec((frames, pair), lambda g: (0, g))
    return pl.pallas_call(
        attend_kernel,
        grid=(width // pair,),
        in_specs=[
            pl.BlockSpec(rec_q.shape, lambda g: (0, 0)),
            pl.BlockSpec(rec_k.shape, lambda g: (0, 0)),
            tile,
        ]
        + [tile] * (2 * NBLK),
        out_specs=tile,
        out_shape=jax.ShapeDtypeStruct((frames, width), jnp.bfloat16),
        scratch_shapes=[pltpu.VMEM((NBLK, frames, frames), jnp.float32)],
    )(rec_q, rec_k, query, *keys, *vals)


def shards(
    features,
    queries,
    key_vectors,
    values,
    record_lengths,
    output_weight,
    norm_gain,
    norm_bias,
    depthwise_taps,
    conv_gain,
    conv_bias,
    pointwise_weight,
):
    frames = features.shape[0]
    per_group = lax.axis_size("blk")
    nblocks = lax.axis_size("grp") * per_group
    block_here = lax.axis_index("grp") * per_group + lax.axis_index("blk")
    rec_ends = jnp.cumsum(record_lengths)
    starts = rec_ends - record_lengths
    offsets = jnp.arange(frames, dtype=jnp.int32)
    own_rec = segment_of(block_here * frames + offsets, starts)

    def hop(pair, distance):
        return tuple(shifted_2(x, ("grp", "blk"), distance) for x in pair)

    own_pair = (key_vectors, values)
    from_m2 = hop(own_pair, 2)
    from_p2 = hop(own_pair, -2)
    from_m4 = hop(from_m2, 2)
    from_p4 = hop(from_p2, -2)
    parity = block_here % 2
    partner = block_here + 1 - 2 * parity
    far = tuple(lax.select(parity == 0, p4, m4) for m4, p4 in zip(from_m4, from_p4))
    swap = [(i, i ^ 1) for i in range(nblocks)]
    got = [
        tuple(lax.ppermute(x, ("grp", "blk"), swap) for x in pair)
        for pair in (own_pair, from_m2, from_p2, far)
    ]
    pairs = [own_pair, from_m2, from_p2, from_m4, from_p4] + got
    key_blocks = jnp.stack([
        block_here, block_here - 2, block_here + 2, block_here - 4, block_here + 4,
        partner, partner - 2, partner + 2, partner - 4 + 8 * parity,
    ]).astype(jnp.int32)
    key_pos = (key_blocks[:, None] * frames + offsets[None, :]).reshape(-1)
    key_inside = ((key_blocks >= 0) & (key_blocks < nblocks))[:, None]
    key_rec = jnp.where(key_inside, segment_of(key_pos, starts).reshape(NBLK, frames), -1)
    rows = -(-NBLK // 8) * 8
    key_rec = jnp.pad(key_rec, ((0, rows - NBLK), (0, 0)), constant_values=-1)
    keys = [p[0] for p in pairs]
    vals = [p[1] for p in pairs]
    attended = attend(own_rec[:, None], key_rec, queries, keys, vals)
    projected = jnp.dot(attended, output_weight, preferred_element_type=jnp.float32)
    resid = lax.optimization_barrier(
        (features.astype(jnp.float32) + projected).astype(jnp.bfloat16)
    )
    resid32 = resid.astype(jnp.float32)
    center = jnp.mean(resid32, axis=1, keepdims=True)
    spread = jnp.mean((resid32 - center) ** 2, axis=1, keepdims=True)
    normed = ((resid32 - center) * lax.rsqrt(spread + 1e-05) * norm_gain + norm_bias).astype(
        jnp.bfloat16
    )
    rim_width = (depthwise_taps.shape[0] - 1) // 2
    extended = padded(normed, ((("grp", "blk"), 0),), rim_width)
    ext_positions = (
        block_here * frames - rim_width + jnp.arange(frames + 2 * rim_width, dtype=jnp.int32)
    )
    ext_inside = (ext_positions >= 0) & (ext_positions < nblocks * frames)
    ext_rec = jnp.where(ext_inside, segment_of(ext_positions, starts), -1)
    extended32 = lax.optimization_barrier(extended).astype(jnp.float32)
    summed = jnp.zeros((frames, normed.shape[1]), jnp.float32)
    for tap in range(depthwise_taps.shape[0]):
        same_rec = (ext_rec[tap : tap + frames] == own_rec)[:, None]
        summed = summed + jnp.where(
            same_rec, extended32[tap : tap + frames] * depthwise_taps[tap], 0.0
        )
    shifted = summed * conv_gain + conv_bias
    act = lax.optimization_barrier((shifted * jax.nn.sigmoid(shifted)).astype(jnp.bfloat16))
    return (resid32 + jnp.dot(act, pointwise_weight, preferred_element_type=jnp.float32)).astype(
        jnp.bfloat16
    )


def solution(mesh):
    in_specs = (
        P(("grp", "blk"), None),
        P(("grp", "blk"), None),
        P(("grp", "blk"), None),
        P(("grp", "blk"), None),
        P(),
        P(),
        P(),
        P(),
        P(),
        P(),
        P(),
        P(),
    )
    out_specs = P(("grp", "blk"), None)
    return jax.shard_map(shards, mesh=mesh, in_specs=in_specs, out_specs=out_specs, check_vma=False)
```

```python
import functools

import jax
import jax.numpy as jnp
from jax import lax
from jax.sharding import PartitionSpec as P
from jax.experimental import pallas as pl
from jax.experimental.pallas import tpu as pltpu

HEADS = 12
HD = 64
REACH = 4


def shifted_2(block, axis, distance):
    devices = range(lax.axis_size(axis))
    route = [(i - distance, i) for i in devices if i - distance in devices]
    return lax.ppermute(block, axis, route)


def padded(block, sides, width):
    for axis, dim in sides:
        count = lax.axis_size(axis)
        forward = [(i, i + 1) for i in range(count - 1)]
        backward = [(target, source) for source, target in forward]
        low = lax.ppermute(
            lax.slice_in_dim(block, block.shape[dim] - width, None, axis=dim), axis, forward
        )
        high = lax.ppermute(lax.slice_in_dim(block, 0, width, axis=dim), axis, backward)
        block = jnp.concatenate([low, block, high], axis=dim)
    return block


def segment_of(positions, starts):
    return jnp.sum((starts[None, :] <= positions[:, None]).astype(jnp.int32), axis=1) - 1


def from_before(moving):
    return shifted_2(moving, ("grp", "blk"), 1)


def from_after(moving):
    return shifted_2(moving, ("grp", "blk"), -1)


NBLK = 2 * REACH + 1


def absorb_kernel(nblk, final, recq_ref, reck_ref, q_ref, m_ref, l_ref, acc_ref, *refs):
    k_refs = refs[:nblk]
    v_refs = refs[nblk : 2 * nblk]
    m_out, l_out, acc_out, s_scr = refs[2 * nblk :]
    rec_q = recq_ref[...]
    for hh in range(2):
        cols = slice(hh * HD, (hh + 1) * HD)
        q_h = q_ref[:, cols]
        m_old = m_ref[0, :, hh : hh + 1]
        top = m_old
        for j in range(nblk):
            s = lax.dot_general(
                q_h, k_refs[j][:, cols], (((1,), (1,)), ((), ())),
                preferred_element_type=jnp.float32,
            ) * (HD ** (-0.5))
            s = jnp.where(rec_q == reck_ref[j : j + 1, :], s, -1e30)
            s_scr[j] = s
            top = jnp.maximum(top, jnp.max(s, axis=1, keepdims=True))
        alpha = jnp.exp(m_old - top)
        total = l_ref[0, :, hh : hh + 1] * alpha
        acc = acc_ref[:, cols] * alpha
        for j in range(nblk):
            p = jnp.exp(s_scr[j] - top)
            total = total + jnp.sum(p, axis=1, keepdims=True)
            acc = acc + jnp.dot(p.astype(jnp.bfloat16), v_refs[j][:, cols],
                                preferred_element_type=jnp.float32)
        if final:
            acc_out[:, cols] = (acc / total).astype(acc_out.dtype)
        else:
            acc_out[:, cols] = acc
            m_out[0, :, hh : hh + 1] = top
            l_out[0, :, hh : hh + 1] = total


def absorb(state, rec_q, key_rec, query, keys, vals, final):
    m, l, acc = state
    nblk = len(keys)
    frames, width = query.shape
    pair = 2 * HD
    steps = width // pair
    rows = -(-nblk // 8) * 8
    rec_k = jnp.pad(key_rec, ((0, rows - nblk), (0, 0)), constant_values=-1)
    tile = pl.BlockSpec((frames, pair), lambda g: (0, g))
    stat = pl.BlockSpec((1, frames, 2), lambda g: (g, 0, 0))
    out_dtype = jnp.bfloat16 if final else jnp.float32
    out = pl.pallas_call(
        functools.partial(absorb_kernel, nblk, final),
        grid=(steps,),
        in_specs=[
            pl.BlockSpec(rec_q.shape, lambda g: (0, 0)),
            pl.BlockSpec(rec_k.shape, lambda g: (0, 0)),
            tile, stat, stat, tile,
        ]
        + [tile] * (2 * nblk),
        out_specs=[stat, stat, tile],
        out_shape=[
            jax.ShapeDtypeStruct(m.shape, jnp.float32),
            jax.ShapeDtypeStruct(l.shape, jnp.float32),
            jax.ShapeDtypeStruct((frames, width), out_dtype),
        ],
        scratch_shapes=[pltpu.VMEM((nblk, frames, frames), jnp.float32)],
    )(rec_q, rec_k, query, m, l, acc, *keys, *vals)
    return tuple(out)


def shards(
    features,
    queries,
    key_vectors,
    values,
    record_lengths,
    output_weight,
    norm_gain,
    norm_bias,
    depthwise_taps,
    conv_gain,
    conv_bias,
    pointwise_weight,
):
    frames = features.shape[0]
    per_group = lax.axis_size("blk")
    nblocks = lax.axis_size("grp") * per_group
    block_here = lax.axis_index("grp") * per_group + lax.axis_index("blk")
    rec_ends = jnp.cumsum(record_lengths)
    starts = rec_ends - record_lengths
    offsets = jnp.arange(frames, dtype=jnp.int32)
    own_rec = segment_of(block_here * frames + offsets, starts)

    def hop(pair, distance):
        return tuple(shifted_2(x, ("grp", "blk"), distance) for x in pair)

    own_pair = (key_vectors, values)
    from_m2 = hop(own_pair, 2)
    from_p2 = hop(own_pair, -2)
    from_m4 = hop(from_m2, 2)
    from_p4 = hop(from_p2, -2)
    parity = block_here % 2
    partner = block_here + 1 - 2 * parity
    far = tuple(lax.select(parity == 0, p4, m4) for m4, p4 in zip(from_m4, from_p4))
    swap = [(i, i ^ 1) for i in range(nblocks)]
    got = [
        tuple(lax.ppermute(x, ("grp", "blk"), swap) for x in pair)
        for pair in (own_pair, from_m2, from_p2, far)
    ]
    def recs_of(blocks):
        blocks = jnp.stack(blocks).astype(jnp.int32)
        pos = (blocks[:, None] * frames + offsets[None, :]).reshape(-1)
        inside = ((blocks >= 0) & (blocks < nblocks))[:, None]
        return jnp.where(inside, segment_of(pos, starts).reshape(blocks.shape[0], frames), -1)

    stages = [
        ([own_pair], [block_here]),
        (
            [from_m2, from_p2] + got[:3],
            [block_here - 2, block_here + 2, partner, partner - 2, partner + 2],
        ),
        ([from_m4, from_p4, got[3]], [block_here - 4, block_here + 4, partner - 4 + 8 * parity]),
    ]
    steps = queries.shape[1] // (2 * HD)
    state = (
        jnp.full((steps, frames, 2), -1e30, jnp.float32),
        jnp.zeros((steps, frames, 2), jnp.float32),
        jnp.zeros(queries.shape, jnp.float32),
    )
    rec_q = own_rec[:, None]
    for n, (stage_pairs, blocks) in enumerate(stages):
        state = absorb(
            state, rec_q, recs_of(blocks), queries,
            [p[0] for p in stage_pairs], [p[1] for p in stage_pairs],
            n == len(stages) - 1,
        )
    attended = state[2]
    projected = jnp.dot(attended, output_weight, preferred_element_type=jnp.float32)
    resid = lax.optimization_barrier(
        (features.astype(jnp.float32) + projected).astype(jnp.bfloat16)
    )
    resid32 = resid.astype(jnp.float32)
    center = jnp.mean(resid32, axis=1, keepdims=True)
    spread = jnp.mean((resid32 - center) ** 2, axis=1, keepdims=True)
    normed = ((resid32 - center) * lax.rsqrt(spread + 1e-05) * norm_gain + norm_bias).astype(
        jnp.bfloat16
    )
    rim_width = (depthwise_taps.shape[0] - 1) // 2
    extended = padded(normed, ((("grp", "blk"), 0),), rim_width)
    ext_positions = (
        block_here * frames - rim_width + jnp.arange(frames + 2 * rim_width, dtype=jnp.int32)
    )
    ext_inside = (ext_positions >= 0) & (ext_positions < nblocks * frames)
    ext_rec = jnp.where(ext_inside, segment_of(ext_positions, starts), -1)
    extended32 = lax.optimization_barrier(extended).astype(jnp.float32)
    summed = jnp.zeros((frames, normed.shape[1]), jnp.float32)
    for tap in range(depthwise_taps.shape[0]):
        same_rec = (ext_rec[tap : tap + frames] == own_rec)[:, None]
        summed = summed + jnp.where(
            same_rec, extended32[tap : tap + frames] * depthwise_taps[tap], 0.0
        )
    shifted = summed * conv_gain + conv_bias
    act = lax.optimization_barrier((shifted * jax.nn.sigmoid(shifted)).astype(jnp.bfloat16))
    return (resid32 + jnp.dot(act, pointwise_weight, preferred_element_type=jnp.float32)).astype(
        jnp.bfloat16
    )


def solution(mesh):
    in_specs = (
        P(("grp", "blk"), None),
        P(("grp", "blk"), None),
        P(("grp", "blk"), None),
        P(("grp", "blk"), None),
        P(),
        P(),
        P(),
        P(),
        P(),
        P(),
        P(),
        P(),
    )
    out_specs = P(("grp", "blk"), None)
    return jax.shard_map(shards, mesh=mesh, in_specs=in_specs, out_specs=out_specs, check_vma=False)
```

```python
import jax
import jax.numpy as jnp
from jax import lax
from jax.sharding import PartitionSpec as P
from jax.experimental import pallas as pl
from jax.experimental.pallas import tpu as pltpu

HEADS = 12
HD = 64
REACH = 4


def shifted_2(block, axis, distance):
    devices = range(lax.axis_size(axis))
    route = [(i - distance, i) for i in devices if i - distance in devices]
    return lax.ppermute(block, axis, route)


def padded(block, sides, width):
    for axis, dim in sides:
        count = lax.axis_size(axis)
        forward = [(i, i + 1) for i in range(count - 1)]
        backward = [(target, source) for source, target in forward]
        low = lax.ppermute(
            lax.slice_in_dim(block, block.shape[dim] - width, None, axis=dim), axis, forward
        )
        high = lax.ppermute(lax.slice_in_dim(block, 0, width, axis=dim), axis, backward)
        block = jnp.concatenate([low, block, high], axis=dim)
    return block


def segment_of(positions, starts):
    return jnp.sum((starts[None, :] <= positions[:, None]).astype(jnp.int32), axis=1) - 1


def from_before(moving):
    return shifted_2(moving, ("grp", "blk"), 1)


def from_after(moving):
    return shifted_2(moving, ("grp", "blk"), -1)


NBLK = 2 * REACH + 1


def fold_lanes(x, op):
    width = x.shape[1]
    out = x[:, :128]
    for c in range(128, width, 128):
        out = op(out, x[:, c : c + 128])
    return out


def attend_kernel(recq_ref, reck_ref, q_ref, *refs):
    k_refs = refs[:NBLK]
    v_refs = refs[NBLK : 2 * NBLK]
    out_ref = refs[2 * NBLK]
    s_scr, bias_scr = refs[2 * NBLK + 1 :]

    @pl.when(pl.program_id(0) == 0)
    def _():
        rec_q = recq_ref[...]
        for j in range(NBLK):
            bias_scr[j] = jnp.where(rec_q == reck_ref[j : j + 1, :], 0.0, -1e30)

    for hh in range(2):
        cols = slice(hh * HD, (hh + 1) * HD)
        q_h = q_ref[:, cols]
        wide_top = None
        for j in range(NBLK):
            s = lax.dot_general(
                q_h, k_refs[j][:, cols], (((1,), (1,)), ((), ())),
                preferred_element_type=jnp.float32,
            ) * (HD ** (-0.5)) + bias_scr[j]
            s_scr[j] = s
            part = fold_lanes(s, jnp.maximum)
            wide_top = part if wide_top is None else jnp.maximum(wide_top, part)
        top = jnp.max(wide_top, axis=1, keepdims=True)
        wide_total = None
        acc = None
        for j in range(NBLK):
            p = jnp.exp(s_scr[j] - top)
            part = fold_lanes(p, jnp.add)
            prod = jnp.dot(p.astype(jnp.bfloat16), v_refs[j][:, cols],
                           preferred_element_type=jnp.float32)
            wide_total = part if wide_total is None else wide_total + part
            acc = prod if acc is None else acc + prod
        total = jnp.sum(wide_total, axis=1, keepdims=True)
        out_ref[:, cols] = (acc / total).astype(out_ref.dtype)


def attend(rec_q, rec_k, query, keys, vals):
    frames, width = query.shape
    pair = 2 * HD
    tile = pl.BlockSpec((frames, pair), lambda g: (0, g))
    return pl.pallas_call(
        attend_kernel,
        grid=(width // pair,),
        in_specs=[
            pl.BlockSpec(rec_q.shape, lambda g: (0, 0)),
            pl.BlockSpec(rec_k.shape, lambda g: (0, 0)),
            tile,
        ]
        + [tile] * (2 * NBLK),
        out_specs=tile,
        out_shape=jax.ShapeDtypeStruct((frames, width), jnp.bfloat16),
        scratch_shapes=[pltpu.VMEM((NBLK, frames, frames), jnp.float32)] * 2,
    )(rec_q, rec_k, query, *keys, *vals)


def shards(
    features,
    queries,
    key_vectors,
    values,
    record_lengths,
    output_weight,
    norm_gain,
    norm_bias,
    depthwise_taps,
    conv_gain,
    conv_bias,
    pointwise_weight,
):
    frames = features.shape[0]
    per_group = lax.axis_size("blk")
    nblocks = lax.axis_size("grp") * per_group
    block_here = lax.axis_index("grp") * per_group + lax.axis_index("blk")
    rec_ends = jnp.cumsum(record_lengths)
    starts = rec_ends - record_lengths
    offsets = jnp.arange(frames, dtype=jnp.int32)
    own_rec = segment_of(block_here * frames + offsets, starts)

    def hop(pair, distance):
        return tuple(shifted_2(x, ("grp", "blk"), distance) for x in pair)

    own_pair = (key_vectors, values)
    from_m2 = hop(own_pair, 2)
    from_p2 = hop(own_pair, -2)
    from_m4 = hop(from_m2, 2)
    from_p4 = hop(from_p2, -2)
    parity = block_here % 2
    partner = block_here + 1 - 2 * parity
    far = tuple(lax.select(parity == 0, p4, m4) for m4, p4 in zip(from_m4, from_p4))
    swap = [(i, i ^ 1) for i in range(nblocks)]
    got = [
        tuple(lax.ppermute(x, ("grp", "blk"), swap) for x in pair)
        for pair in (own_pair, from_m2, from_p2, far)
    ]
    pairs = [own_pair, from_m2, from_p2, from_m4, from_p4] + got
    key_blocks = jnp.stack([
        block_here, block_here - 2, block_here + 2, block_here - 4, block_here + 4,
        partner, partner - 2, partner + 2, partner - 4 + 8 * parity,
    ]).astype(jnp.int32)
    key_pos = (key_blocks[:, None] * frames + offsets[None, :]).reshape(-1)
    key_inside = ((key_blocks >= 0) & (key_blocks < nblocks))[:, None]
    key_rec = jnp.where(key_inside, segment_of(key_pos, starts).reshape(NBLK, frames), -1)
    rows = -(-NBLK // 8) * 8
    key_rec = jnp.pad(key_rec, ((0, rows - NBLK), (0, 0)), constant_values=-1)
    keys = [p[0] for p in pairs]
    vals = [p[1] for p in pairs]
    attended = attend(own_rec[:, None], key_rec, queries, keys, vals)
    projected = jnp.dot(attended, output_weight, preferred_element_type=jnp.float32)
    resid = lax.optimization_barrier(
        (features.astype(jnp.float32) + projected).astype(jnp.bfloat16)
    )
    resid32 = resid.astype(jnp.float32)
    center = jnp.mean(resid32, axis=1, keepdims=True)
    spread = jnp.mean((resid32 - center) ** 2, axis=1, keepdims=True)
    normed = ((resid32 - center) * lax.rsqrt(spread + 1e-05) * norm_gain + norm_bias).astype(
        jnp.bfloat16
    )
    rim_width = (depthwise_taps.shape[0] - 1) // 2
    extended = padded(normed, ((("grp", "blk"), 0),), rim_width)
    ext_positions = (
        block_here * frames - rim_width + jnp.arange(frames + 2 * rim_width, dtype=jnp.int32)
    )
    ext_inside = (ext_positions >= 0) & (ext_positions < nblocks * frames)
    ext_rec = jnp.where(ext_inside, segment_of(ext_positions, starts), -1)
    extended32 = lax.optimization_barrier(extended).astype(jnp.float32)
    summed = jnp.zeros((frames, normed.shape[1]), jnp.float32)
    for tap in range(depthwise_taps.shape[0]):
        same_rec = (ext_rec[tap : tap + frames] == own_rec)[:, None]
        summed = summed + jnp.where(
            same_rec, extended32[tap : tap + frames] * depthwise_taps[tap], 0.0
        )
    shifted = summed * conv_gain + conv_bias
    act = lax.optimization_barrier((shifted * jax.nn.sigmoid(shifted)).astype(jnp.bfloat16))
    return (resid32 + jnp.dot(act, pointwise_weight, preferred_element_type=jnp.float32)).astype(
        jnp.bfloat16
    )


def solution(mesh):
    in_specs = (
        P(("grp", "blk"), None),
        P(("grp", "blk"), None),
        P(("grp", "blk"), None),
        P(("grp", "blk"), None),
        P(),
        P(),
        P(),
        P(),
        P(),
        P(),
        P(),
        P(),
    )
    out_specs = P(("grp", "blk"), None)
    return jax.shard_map(shards, mesh=mesh, in_specs=in_specs, out_specs=out_specs, check_vma=False)
```

```python
import jax
import jax.numpy as jnp
from jax import lax
from jax.sharding import PartitionSpec as P
from jax.experimental import pallas as pl
from jax.experimental.pallas import tpu as pltpu

HEADS = 12
HD = 64
REACH = 4


def shifted_2(block, axis, distance):
    devices = range(lax.axis_size(axis))
    route = [(i - distance, i) for i in devices if i - distance in devices]
    return lax.ppermute(block, axis, route)


def padded(block, sides, width):
    for axis, dim in sides:
        count = lax.axis_size(axis)
        forward = [(i, i + 1) for i in range(count - 1)]
        backward = [(target, source) for source, target in forward]
        low = lax.ppermute(
            lax.slice_in_dim(block, block.shape[dim] - width, None, axis=dim), axis, forward
        )
        high = lax.ppermute(lax.slice_in_dim(block, 0, width, axis=dim), axis, backward)
        block = jnp.concatenate([low, block, high], axis=dim)
    return block


def segment_of(positions, starts):
    return jnp.sum((starts[None, :] <= positions[:, None]).astype(jnp.int32), axis=1) - 1


def from_before(moving):
    return shifted_2(moving, ("grp", "blk"), 1)


def from_after(moving):
    return shifted_2(moving, ("grp", "blk"), -1)


NBLK = 2 * REACH + 1


def fold_lanes(x, op):
    width = x.shape[1]
    out = x[:, :128]
    for c in range(128, width, 128):
        out = op(out, x[:, c : c + 128])
    return out


def attend_kernel(recq_ref, reck_ref, q_ref, *refs):
    k_refs = refs[:NBLK]
    v_refs = refs[NBLK : 2 * NBLK]
    out_ref = refs[2 * NBLK]
    s_scr, bias_scr = refs[2 * NBLK + 1 :]

    @pl.when(pl.program_id(0) == 0)
    def _():
        rec_q = recq_ref[...]
        for j in range(NBLK):
            bias_scr[j] = jnp.where(rec_q == reck_ref[j : j + 1, :], 0.0, -1e30)

    for hh in range(2):
        cols = slice(hh * HD, (hh + 1) * HD)
        q_h = q_ref[:, cols]
        wide_top = None
        for j in range(NBLK):
            s = lax.dot_general(
                q_h, k_refs[j][:, cols], (((1,), (1,)), ((), ())),
                preferred_element_type=jnp.float32,
            ) * (HD ** (-0.5)) + bias_scr[j]
            s_scr[j] = s
            part = fold_lanes(s, jnp.maximum)
            wide_top = part if wide_top is None else jnp.maximum(wide_top, part)
        top = jnp.max(wide_top, axis=1, keepdims=True)
        wide_total = None
        acc = None
        for j in range(NBLK):
            p = jnp.exp(s_scr[j] - top)
            part = fold_lanes(p, jnp.add)
            prod = jnp.dot(p.astype(jnp.bfloat16), v_refs[j][:, cols],
                           preferred_element_type=jnp.float32)
            wide_total = part if wide_total is None else wide_total + part
            acc = prod if acc is None else acc + prod
        total = jnp.sum(wide_total, axis=1, keepdims=True)
        out_ref[:, cols] = (acc / total).astype(out_ref.dtype)


def attend(rec_q, rec_k, query, keys, vals):
    frames, width = query.shape
    pair = 2 * HD
    tile = pl.BlockSpec((frames, pair), lambda g: (0, g))
    return pl.pallas_call(
        attend_kernel,
        grid=(width // pair,),
        in_specs=[
            pl.BlockSpec(rec_q.shape, lambda g: (0, 0)),
            pl.BlockSpec(rec_k.shape, lambda g: (0, 0)),
            tile,
        ]
        + [tile] * (2 * NBLK),
        out_specs=tile,
        out_shape=jax.ShapeDtypeStruct((frames, width), jnp.bfloat16),
        scratch_shapes=[pltpu.VMEM((NBLK, frames, frames), jnp.float32)] * 2,
    )(rec_q, rec_k, query, *keys, *vals)


def shards(
    features,
    queries,
    key_vectors,
    values,
    record_lengths,
    output_weight,
    norm_gain,
    norm_bias,
    depthwise_taps,
    conv_gain,
    conv_bias,
    pointwise_weight,
):
    frames = features.shape[0]
    per_group = lax.axis_size("blk")
    nblocks = lax.axis_size("grp") * per_group
    block_here = lax.axis_index("grp") * per_group + lax.axis_index("blk")
    rec_ends = jnp.cumsum(record_lengths)
    starts = rec_ends - record_lengths
    offsets = jnp.arange(frames, dtype=jnp.int32)
    own_rec = segment_of(block_here * frames + offsets, starts)

    def hop(pair, distance):
        return tuple(shifted_2(x, ("grp", "blk"), distance) for x in pair)

    own_pair = (key_vectors, values)
    from_m2 = hop(own_pair, 2)
    from_p2 = hop(own_pair, -2)
    from_m4 = hop(from_m2, 2)
    from_p4 = hop(from_p2, -2)
    parity = block_here % 2
    partner = block_here + 1 - 2 * parity
    far = tuple(lax.select(parity == 0, p4, m4) for m4, p4 in zip(from_m4, from_p4))
    swap = [(i, i ^ 1) for i in range(nblocks)]
    got = [
        tuple(lax.ppermute(x, ("grp", "blk"), swap) for x in pair)
        for pair in (own_pair, from_m2, from_p2, far)
    ]
    pairs = [own_pair, from_m2, from_p2, from_m4, from_p4] + got
    key_blocks = jnp.stack([
        block_here, block_here - 2, block_here + 2, block_here - 4, block_here + 4,
        partner, partner - 2, partner + 2, partner - 4 + 8 * parity,
    ]).astype(jnp.int32)
    key_pos = (key_blocks[:, None] * frames + offsets[None, :]).reshape(-1)
    key_inside = ((key_blocks >= 0) & (key_blocks < nblocks))[:, None]
    key_rec = jnp.where(key_inside, segment_of(key_pos, starts).reshape(NBLK, frames), -1)
    rows = -(-NBLK // 8) * 8
    key_rec = jnp.pad(key_rec, ((0, rows - NBLK), (0, 0)), constant_values=-1)
    keys = [p[0] for p in pairs]
    vals = [p[1] for p in pairs]
    attended = attend(own_rec[:, None], key_rec, queries, keys, vals)
    projected = jnp.dot(attended, output_weight, preferred_element_type=jnp.float32)
    resid = lax.optimization_barrier(
        (features.astype(jnp.float32) + projected).astype(jnp.bfloat16)
    )
    resid32 = resid.astype(jnp.float32)
    center = jnp.mean(resid32, axis=1, keepdims=True)
    spread = jnp.mean((resid32 - center) ** 2, axis=1, keepdims=True)
    normed = ((resid32 - center) * lax.rsqrt(spread + 1e-05) * norm_gain + norm_bias).astype(
        jnp.bfloat16
    )
    rim_width = (depthwise_taps.shape[0] - 1) // 2
    head_rows = normed[:rim_width]
    tail_rows = normed[frames - rim_width :]
    cross = [(i, i + 1) for i in range(1, nblocks - 1, 2)]
    cross = cross + [(j, i) for i, j in cross]
    over_link = lax.ppermute(
        lax.select(parity == 0, head_rows, tail_rows), ("grp", "blk"), cross
    )
    on_chip = lax.ppermute(
        lax.select(parity == 0, tail_rows, head_rows), ("grp", "blk"), swap
    )
    low = lax.select(parity == 0, over_link, on_chip)
    high = lax.select(parity == 0, on_chip, over_link)
    extended = jnp.concatenate([low, normed, high], axis=0)
    ext_positions = (
        block_here * frames - rim_width + jnp.arange(frames + 2 * rim_width, dtype=jnp.int32)
    )
    ext_inside = (ext_positions >= 0) & (ext_positions < nblocks * frames)
    ext_rec = jnp.where(ext_inside, segment_of(ext_positions, starts), -1)
    extended32 = lax.optimization_barrier(extended).astype(jnp.float32)
    summed = jnp.zeros((frames, normed.shape[1]), jnp.float32)
    for tap in range(depthwise_taps.shape[0]):
        same_rec = (ext_rec[tap : tap + frames] == own_rec)[:, None]
        summed = summed + jnp.where(
            same_rec, extended32[tap : tap + frames] * depthwise_taps[tap], 0.0
        )
    shifted = summed * conv_gain + conv_bias
    act = lax.optimization_barrier((shifted * jax.nn.sigmoid(shifted)).astype(jnp.bfloat16))
    return (resid32 + jnp.dot(act, pointwise_weight, preferred_element_type=jnp.float32)).astype(
        jnp.bfloat16
    )


def solution(mesh):
    in_specs = (
        P(("grp", "blk"), None),
        P(("grp", "blk"), None),
        P(("grp", "blk"), None),
        P(("grp", "blk"), None),
        P(),
        P(),
        P(),
        P(),
        P(),
        P(),
        P(),
        P(),
    )
    out_specs = P(("grp", "blk"), None)
    return jax.shard_map(shards, mesh=mesh, in_specs=in_specs, out_specs=out_specs, check_vma=False)
```

```python
import jax
import jax.numpy as jnp
from jax import lax
from jax.sharding import PartitionSpec as P
from jax.experimental import pallas as pl
from jax.experimental.pallas import tpu as pltpu

HEADS = 12
HD = 64
REACH = 4


def shifted_2(block, axis, distance):
    devices = range(lax.axis_size(axis))
    route = [(i - distance, i) for i in devices if i - distance in devices]
    return lax.ppermute(block, axis, route)


def padded(block, sides, width):
    for axis, dim in sides:
        count = lax.axis_size(axis)
        forward = [(i, i + 1) for i in range(count - 1)]
        backward = [(target, source) for source, target in forward]
        low = lax.ppermute(
            lax.slice_in_dim(block, block.shape[dim] - width, None, axis=dim), axis, forward
        )
        high = lax.ppermute(lax.slice_in_dim(block, 0, width, axis=dim), axis, backward)
        block = jnp.concatenate([low, block, high], axis=dim)
    return block


def segment_of(positions, starts):
    return jnp.sum((starts[None, :] <= positions[:, None]).astype(jnp.int32), axis=1) - 1


def from_before(moving):
    return shifted_2(moving, ("grp", "blk"), 1)


def from_after(moving):
    return shifted_2(moving, ("grp", "blk"), -1)


NBLK = 2 * REACH + 1


def fold_lanes(x, op):
    width = x.shape[1]
    out = x[:, :128]
    for c in range(128, width, 128):
        out = op(out, x[:, c : c + 128])
    return out


def attend_kernel(recq_ref, reck_ref, q_ref, *refs):
    k_refs = refs[:NBLK]
    v_refs = refs[NBLK : 2 * NBLK]
    out_ref = refs[2 * NBLK]
    s_scr, bias_scr = refs[2 * NBLK + 1 :]

    @pl.when(pl.program_id(0) == 0)
    def _():
        rec_q = recq_ref[...]
        for j in range(NBLK):
            bias_scr[j] = jnp.where(rec_q == reck_ref[j : j + 1, :], 0.0, -1e30)

    for hh in range(2):
        cols = slice(hh * HD, (hh + 1) * HD)
        q_h = q_ref[:, cols]
        wide_top = None
        for j in range(NBLK):
            s = lax.dot_general(
                q_h, k_refs[j][:, cols], (((1,), (1,)), ((), ())),
                preferred_element_type=jnp.float32,
            ) * (HD ** (-0.5)) + bias_scr[j]
            s_scr[j] = s
            part = fold_lanes(s, jnp.maximum)
            wide_top = part if wide_top is None else jnp.maximum(wide_top, part)
        top = jnp.max(wide_top, axis=1, keepdims=True)
        wide_total = None
        acc = None
        for j in range(NBLK):
            p = jnp.exp(s_scr[j] - top)
            part = fold_lanes(p, jnp.add)
            prod = jnp.dot(p.astype(jnp.bfloat16), v_refs[j][:, cols],
                           preferred_element_type=jnp.float32)
            wide_total = part if wide_total is None else wide_total + part
            acc = prod if acc is None else acc + prod
        total = jnp.sum(wide_total, axis=1, keepdims=True)
        out_ref[:, cols] = (acc / total).astype(out_ref.dtype)


def attend(rec_q, rec_k, query, keys, vals):
    frames, width = query.shape
    pair = 2 * HD
    tile = pl.BlockSpec((frames, pair), lambda g: (0, g))
    return pl.pallas_call(
        attend_kernel,
        grid=(width // pair,),
        in_specs=[
            pl.BlockSpec(rec_q.shape, lambda g: (0, 0)),
            pl.BlockSpec(rec_k.shape, lambda g: (0, 0)),
            tile,
        ]
        + [tile] * (2 * NBLK),
        out_specs=tile,
        out_shape=jax.ShapeDtypeStruct((frames, width), jnp.bfloat16),
        scratch_shapes=[pltpu.VMEM((NBLK, frames, frames), jnp.float32)] * 2,
    )(rec_q, rec_k, query, *keys, *vals)


def shards(
    features,
    queries,
    key_vectors,
    values,
    record_lengths,
    output_weight,
    norm_gain,
    norm_bias,
    depthwise_taps,
    conv_gain,
    conv_bias,
    pointwise_weight,
):
    frames = features.shape[0]
    per_group = lax.axis_size("blk")
    nblocks = lax.axis_size("grp") * per_group
    block_here = lax.axis_index("grp") * per_group + lax.axis_index("blk")
    rec_ends = jnp.cumsum(record_lengths)
    starts = rec_ends - record_lengths
    offsets = jnp.arange(frames, dtype=jnp.int32)
    own_rec = segment_of(block_here * frames + offsets, starts)

    def hop(pair, distance):
        return tuple(shifted_2(x, ("grp", "blk"), distance) for x in pair)

    own_pair = (key_vectors, values)
    from_m2 = hop(own_pair, 2)
    from_p2 = hop(own_pair, -2)
    from_m4 = hop(from_m2, 2)
    from_p4 = hop(from_p2, -2)
    parity = block_here % 2
    partner = block_here + 1 - 2 * parity
    far = tuple(lax.select(parity == 0, p4, m4) for m4, p4 in zip(from_m4, from_p4))
    swap = [(i, i ^ 1) for i in range(nblocks)]
    got = [
        tuple(lax.ppermute(x, ("grp", "blk"), swap) for x in pair)
        for pair in (own_pair, from_m2, from_p2, far)
    ]
    pairs = [own_pair, from_m2, from_p2, from_m4, from_p4] + got
    key_blocks = jnp.stack([
        block_here, block_here - 2, block_here + 2, block_here - 4, block_here + 4,
        partner, partner - 2, partner + 2, partner - 4 + 8 * parity,
    ]).astype(jnp.int32)
    key_pos = (key_blocks[:, None] * frames + offsets[None, :]).reshape(-1)
    key_inside = ((key_blocks >= 0) & (key_blocks < nblocks))[:, None]
    key_rec = jnp.where(key_inside, segment_of(key_pos, starts).reshape(NBLK, frames), -1)
    rows = -(-NBLK // 8) * 8
    key_rec = jnp.pad(key_rec, ((0, rows - NBLK), (0, 0)), constant_values=-1)
    keys = [p[0] for p in pairs]
    vals = [p[1] for p in pairs]
    attended = attend(own_rec[:, None], key_rec, queries, keys, vals)
    projected = jnp.dot(attended, output_weight, preferred_element_type=jnp.float32)
    resid = lax.optimization_barrier(
        (features.astype(jnp.float32) + projected).astype(jnp.bfloat16)
    )
    resid32 = resid.astype(jnp.float32)
    center = jnp.mean(resid32, axis=1, keepdims=True)
    spread = jnp.mean((resid32 - center) ** 2, axis=1, keepdims=True)
    normed = ((resid32 - center) * lax.rsqrt(spread + 1e-05) * norm_gain + norm_bias).astype(
        jnp.bfloat16
    )
    rim_width = (depthwise_taps.shape[0] - 1) // 2
    ntaps = depthwise_taps.shape[0]

    def conv_rows(source32, source_rec, out_rec):
        n = out_rec.shape[0]
        summed = jnp.zeros((n, normed.shape[1]), jnp.float32)
        for tap in range(ntaps):
            same_rec = (source_rec[tap : tap + n] == out_rec)[:, None]
            summed = summed + jnp.where(
                same_rec, source32[tap : tap + n] * depthwise_taps[tap], 0.0
            )
        shifted = summed * conv_gain + conv_bias
        return (shifted * jax.nn.sigmoid(shifted)).astype(jnp.bfloat16)

    normed32 = normed.astype(jnp.float32)
    act_mid = conv_rows(normed32, own_rec, own_rec[rim_width : frames - rim_width])
    act_mid, head_rows, tail_rows = lax.optimization_barrier(
        (act_mid, normed[: 2 * rim_width], normed[frames - 2 * rim_width :])
    )
    cross = [(i, i + 1) for i in range(1, nblocks - 1, 2)]
    cross = cross + [(j, i) for i, j in cross]
    over_link = lax.ppermute(
        lax.select(parity == 0, head_rows[:rim_width], tail_rows[rim_width:]), ("grp", "blk"), cross
    )
    on_chip = lax.ppermute(
        lax.select(parity == 0, tail_rows[rim_width:], head_rows[:rim_width]), ("grp", "blk"), swap
    )
    low = lax.select(parity == 0, over_link, on_chip)
    high = lax.select(parity == 0, on_chip, over_link)
    ext_positions = (
        block_here * frames - rim_width + jnp.arange(frames + 2 * rim_width, dtype=jnp.int32)
    )
    ext_inside = (ext_positions >= 0) & (ext_positions < nblocks * frames)
    ext_rec = jnp.where(ext_inside, segment_of(ext_positions, starts), -1)
    edge = 3 * rim_width
    lo_src = jnp.concatenate([low, head_rows], axis=0).astype(jnp.float32)
    hi_src = jnp.concatenate([tail_rows, high], axis=0).astype(jnp.float32)
    act_lo = conv_rows(lo_src, ext_rec[:edge], own_rec[:rim_width])
    act_hi = conv_rows(hi_src, ext_rec[-edge:], own_rec[frames - rim_width :])
    act = jnp.concatenate([act_lo, act_mid, act_hi], axis=0)
    return (resid32 + jnp.dot(act, pointwise_weight, preferred_element_type=jnp.float32)).astype(
        jnp.bfloat16
    )


def solution(mesh):
    in_specs = (
        P(("grp", "blk"), None),
        P(("grp", "blk"), None),
        P(("grp", "blk"), None),
        P(("grp", "blk"), None),
        P(),
        P(),
        P(),
        P(),
        P(),
        P(),
        P(),
        P(),
    )
    out_specs = P(("grp", "blk"), None)
    return jax.shard_map(shards, mesh=mesh, in_specs=in_specs, out_specs=out_specs, check_vma=False)
```

```python
import jax
import jax.numpy as jnp
from jax import lax
from jax.sharding import PartitionSpec as P
from jax.experimental import pallas as pl
from jax.experimental.pallas import tpu as pltpu

HEADS = 12
HD = 64
REACH = 4


def shifted_2(block, axis, distance):
    devices = range(lax.axis_size(axis))
    route = [(i - distance, i) for i in devices if i - distance in devices]
    return lax.ppermute(block, axis, route)


def padded(block, sides, width):
    for axis, dim in sides:
        count = lax.axis_size(axis)
        forward = [(i, i + 1) for i in range(count - 1)]
        backward = [(target, source) for source, target in forward]
        low = lax.ppermute(
            lax.slice_in_dim(block, block.shape[dim] - width, None, axis=dim), axis, forward
        )
        high = lax.ppermute(lax.slice_in_dim(block, 0, width, axis=dim), axis, backward)
        block = jnp.concatenate([low, block, high], axis=dim)
    return block


def segment_of(positions, starts):
    return jnp.sum((starts[None, :] <= positions[:, None]).astype(jnp.int32), axis=1) - 1


def from_before(moving):
    return shifted_2(moving, ("grp", "blk"), 1)


def from_after(moving):
    return shifted_2(moving, ("grp", "blk"), -1)


NBLK = 2 * REACH + 1


def fold_lanes(x, op):
    width = x.shape[1]
    out = x[:, :128]
    for c in range(128, width, 128):
        out = op(out, x[:, c : c + 128])
    return out


def attend_kernel(recq_ref, reck_ref, q_ref, *refs):
    k_refs = refs[:NBLK]
    v_refs = refs[NBLK : 2 * NBLK]
    out_ref = refs[2 * NBLK]
    s_scr, bias_scr = refs[2 * NBLK + 1 :]

    @pl.when(pl.program_id(0) == 0)
    def _():
        rec_q = recq_ref[...]
        for j in range(NBLK):
            bias_scr[j] = jnp.where(rec_q == reck_ref[j : j + 1, :], 0.0, -1e30)

    for hh in range(q_ref.shape[1] // HD):
        cols = slice(hh * HD, (hh + 1) * HD)
        q_h = (q_ref[:, cols].astype(jnp.float32) * (HD ** (-0.5))).astype(q_ref.dtype)
        wide_top = None
        for j in range(NBLK):
            s = lax.dot_general(
                q_h, k_refs[j][:, cols], (((1,), (1,)), ((), ())),
                preferred_element_type=jnp.float32,
            ) + bias_scr[j]
            s_scr[j] = s
            part = fold_lanes(s, jnp.maximum)
            wide_top = part if wide_top is None else jnp.maximum(wide_top, part)
        top = jnp.max(wide_top, axis=1, keepdims=True)
        wide_total = None
        acc = None
        for j in range(NBLK):
            p = jnp.exp(s_scr[j] - top)
            part = fold_lanes(p, jnp.add)
            prod = jnp.dot(p.astype(jnp.bfloat16), v_refs[j][:, cols],
                           preferred_element_type=jnp.float32)
            wide_total = part if wide_total is None else wide_total + part
            acc = prod if acc is None else acc + prod
        total = jnp.sum(wide_total, axis=1, keepdims=True)
        out_ref[:, cols] = (acc / total).astype(out_ref.dtype)


def attend(rec_q, rec_k, query, keys, vals):
    frames, width = query.shape
    pair = 4 * HD
    tile = pl.BlockSpec((frames, pair), lambda g: (0, g))
    return pl.pallas_call(
        attend_kernel,
        grid=(width // pair,),
        in_specs=[
            pl.BlockSpec(rec_q.shape, lambda g: (0, 0)),
            pl.BlockSpec(rec_k.shape, lambda g: (0, 0)),
            tile,
        ]
        + [tile] * (2 * NBLK),
        out_specs=tile,
        out_shape=jax.ShapeDtypeStruct((frames, width), jnp.bfloat16),
        scratch_shapes=[pltpu.VMEM((NBLK, frames, frames), jnp.float32)] * 2,
    )(rec_q, rec_k, query, *keys, *vals)


def shards(
    features,
    queries,
    key_vectors,
    values,
    record_lengths,
    output_weight,
    norm_gain,
    norm_bias,
    depthwise_taps,
    conv_gain,
    conv_bias,
    pointwise_weight,
):
    frames = features.shape[0]
    per_group = lax.axis_size("blk")
    nblocks = lax.axis_size("grp") * per_group
    block_here = lax.axis_index("grp") * per_group + lax.axis_index("blk")
    rec_ends = jnp.cumsum(record_lengths)
    starts = rec_ends - record_lengths
    offsets = jnp.arange(frames, dtype=jnp.int32)
    own_rec = segment_of(block_here * frames + offsets, starts)

    def hop(pair, distance):
        return tuple(shifted_2(x, ("grp", "blk"), distance) for x in pair)

    own_pair = (key_vectors, values)
    from_m2 = hop(own_pair, 2)
    from_p2 = hop(own_pair, -2)
    from_m4 = hop(from_m2, 2)
    from_p4 = hop(from_p2, -2)
    parity = block_here % 2
    partner = block_here + 1 - 2 * parity
    far = tuple(lax.select(parity == 0, p4, m4) for m4, p4 in zip(from_m4, from_p4))
    swap = [(i, i ^ 1) for i in range(nblocks)]
    got = [
        tuple(lax.ppermute(x, ("grp", "blk"), swap) for x in pair)
        for pair in (own_pair, from_m2, from_p2, far)
    ]
    pairs = [own_pair, from_m2, from_p2, from_m4, from_p4] + got
    key_blocks = jnp.stack([
        block_here, block_here - 2, block_here + 2, block_here - 4, block_here + 4,
        partner, partner - 2, partner + 2, partner - 4 + 8 * parity,
    ]).astype(jnp.int32)
    key_pos = (key_blocks[:, None] * frames + offsets[None, :]).reshape(-1)
    key_inside = ((key_blocks >= 0) & (key_blocks < nblocks))[:, None]
    key_rec = jnp.where(key_inside, segment_of(key_pos, starts).reshape(NBLK, frames), -1)
    rows = -(-NBLK // 8) * 8
    key_rec = jnp.pad(key_rec, ((0, rows - NBLK), (0, 0)), constant_values=-1)
    keys = [p[0] for p in pairs]
    vals = [p[1] for p in pairs]
    attended = attend(own_rec[:, None], key_rec, queries, keys, vals)
    projected = jnp.dot(attended, output_weight, preferred_element_type=jnp.float32)
    resid = lax.optimization_barrier(
        (features.astype(jnp.float32) + projected).astype(jnp.bfloat16)
    )
    resid32 = resid.astype(jnp.float32)
    center = jnp.mean(resid32, axis=1, keepdims=True)
    spread = jnp.mean((resid32 - center) ** 2, axis=1, keepdims=True)
    normed = ((resid32 - center) * lax.rsqrt(spread + 1e-05) * norm_gain + norm_bias).astype(
        jnp.bfloat16
    )
    rim_width = (depthwise_taps.shape[0] - 1) // 2
    head_rows = normed[:rim_width]
    tail_rows = normed[frames - rim_width :]
    cross = [(i, i + 1) for i in range(1, nblocks - 1, 2)]
    cross = cross + [(j, i) for i, j in cross]
    over_link = lax.ppermute(
        lax.select(parity == 0, head_rows, tail_rows), ("grp", "blk"), cross
    )
    on_chip = lax.ppermute(
        lax.select(parity == 0, tail_rows, head_rows), ("grp", "blk"), swap
    )
    low = lax.select(parity == 0, over_link, on_chip)
    high = lax.select(parity == 0, on_chip, over_link)
    extended = jnp.concatenate([low, normed, high], axis=0)
    ext_positions = (
        block_here * frames - rim_width + jnp.arange(frames + 2 * rim_width, dtype=jnp.int32)
    )
    ext_inside = (ext_positions >= 0) & (ext_positions < nblocks * frames)
    ext_rec = jnp.where(ext_inside, segment_of(ext_positions, starts), -1)
    extended32 = lax.optimization_barrier(extended).astype(jnp.float32)
    summed = jnp.zeros((frames, normed.shape[1]), jnp.float32)
    for tap in range(depthwise_taps.shape[0]):
        same_rec = (ext_rec[tap : tap + frames] == own_rec)[:, None]
        summed = summed + jnp.where(
            same_rec, extended32[tap : tap + frames] * depthwise_taps[tap], 0.0
        )
    shifted = summed * conv_gain + conv_bias
    act = lax.optimization_barrier((shifted * jax.nn.sigmoid(shifted)).astype(jnp.bfloat16))
    return (resid32 + jnp.dot(act, pointwise_weight, preferred_element_type=jnp.float32)).astype(
        jnp.bfloat16
    )


def solution(mesh):
    in_specs = (
        P(("grp", "blk"), None),
        P(("grp", "blk"), None),
        P(("grp", "blk"), None),
        P(("grp", "blk"), None),
        P(),
        P(),
        P(),
        P(),
        P(),
        P(),
        P(),
        P(),
    )
    out_specs = P(("grp", "blk"), None)
    return jax.shard_map(shards, mesh=mesh, in_specs=in_specs, out_specs=out_specs, check_vma=False)
```

```python
import jax
import jax.numpy as jnp
from jax import lax
from jax.sharding import PartitionSpec as P
from jax.experimental import pallas as pl
from jax.experimental.pallas import tpu as pltpu

HEADS = 12
HD = 64
REACH = 4


def shifted_2(block, axis, distance):
    devices = range(lax.axis_size(axis))
    route = [(i - distance, i) for i in devices if i - distance in devices]
    return lax.ppermute(block, axis, route)


def padded(block, sides, width):
    for axis, dim in sides:
        count = lax.axis_size(axis)
        forward = [(i, i + 1) for i in range(count - 1)]
        backward = [(target, source) for source, target in forward]
        low = lax.ppermute(
            lax.slice_in_dim(block, block.shape[dim] - width, None, axis=dim), axis, forward
        )
        high = lax.ppermute(lax.slice_in_dim(block, 0, width, axis=dim), axis, backward)
        block = jnp.concatenate([low, block, high], axis=dim)
    return block


def segment_of(positions, starts):
    return jnp.sum((starts[None, :] <= positions[:, None]).astype(jnp.int32), axis=1) - 1


def from_before(moving):
    return shifted_2(moving, ("grp", "blk"), 1)


def from_after(moving):
    return shifted_2(moving, ("grp", "blk"), -1)


NBLK = 2 * REACH + 1


def fold_lanes(x, op):
    width = x.shape[1]
    out = x[:, :128]
    for c in range(128, width, 128):
        out = op(out, x[:, c : c + 128])
    return out


def attend_kernel(recq_ref, reck_ref, q_ref, *refs):
    k_refs = refs[:NBLK]
    v_refs = refs[NBLK : 2 * NBLK]
    out_ref = refs[2 * NBLK]
    s_scr, bias_scr = refs[2 * NBLK + 1 :]

    @pl.when(pl.program_id(0) == 0)
    def _():
        rec_q = recq_ref[...]
        for j in range(NBLK):
            bias_scr[j] = jnp.where(rec_q == reck_ref[j : j + 1, :], 0.0, -1e30)

    for hh in range(q_ref.shape[1] // HD):
        cols = slice(hh * HD, (hh + 1) * HD)
        q_h = (q_ref[:, cols].astype(jnp.float32) * (HD ** (-0.5))).astype(q_ref.dtype)
        wide_top = None
        for j in range(NBLK):
            s = lax.dot_general(
                q_h, k_refs[j][:, cols], (((1,), (1,)), ((), ())),
                preferred_element_type=jnp.float32,
            ) + bias_scr[j]
            s_scr[j] = s
            part = fold_lanes(s, jnp.maximum)
            wide_top = part if wide_top is None else jnp.maximum(wide_top, part)
        top = jnp.max(wide_top, axis=1, keepdims=True)
        wide_total = None
        acc = None
        for j in range(NBLK):
            p = jnp.exp(s_scr[j] - top)
            part = fold_lanes(p, jnp.add)
            prod = jnp.dot(p.astype(jnp.bfloat16), v_refs[j][:, cols],
                           preferred_element_type=jnp.float32)
            wide_total = part if wide_total is None else wide_total + part
            acc = prod if acc is None else acc + prod
        total = jnp.sum(wide_total, axis=1, keepdims=True)
        out_ref[:, cols] = (acc / total).astype(out_ref.dtype)


def attend(rec_q, rec_k, query, keys, vals):
    frames, width = query.shape
    pair = 4 * HD
    tile = pl.BlockSpec((frames, pair), lambda g: (0, g))
    v_tile = pl.BlockSpec((frames, pair), lambda g: (0, g + width // pair))
    return pl.pallas_call(
        attend_kernel,
        grid=(width // pair,),
        in_specs=[
            pl.BlockSpec(rec_q.shape, lambda g: (0, 0)),
            pl.BlockSpec(rec_k.shape, lambda g: (0, 0)),
            tile,
        ]
        + [tile] * NBLK
        + [v_tile] * NBLK,
        out_specs=tile,
        out_shape=jax.ShapeDtypeStruct((frames, width), jnp.bfloat16),
        scratch_shapes=[pltpu.VMEM((NBLK, frames, frames), jnp.float32)] * 2,
    )(rec_q, rec_k, query, *keys, *vals)


def shards(
    features,
    queries,
    key_vectors,
    values,
    record_lengths,
    output_weight,
    norm_gain,
    norm_bias,
    depthwise_taps,
    conv_gain,
    conv_bias,
    pointwise_weight,
):
    frames = features.shape[0]
    per_group = lax.axis_size("blk")
    nblocks = lax.axis_size("grp") * per_group
    block_here = lax.axis_index("grp") * per_group + lax.axis_index("blk")
    rec_ends = jnp.cumsum(record_lengths)
    starts = rec_ends - record_lengths
    offsets = jnp.arange(frames, dtype=jnp.int32)
    own_rec = segment_of(block_here * frames + offsets, starts)

    def hop(pair, distance):
        return tuple(shifted_2(x, ("grp", "blk"), distance) for x in pair)

    own_pair = (jnp.concatenate([key_vectors, values], axis=1),)
    from_m2 = hop(own_pair, 2)
    from_p2 = hop(own_pair, -2)
    from_m4 = hop(from_m2, 2)
    from_p4 = hop(from_p2, -2)
    parity = block_here % 2
    partner = block_here + 1 - 2 * parity
    far = tuple(lax.select(parity == 0, p4, m4) for m4, p4 in zip(from_m4, from_p4))
    swap = [(i, i ^ 1) for i in range(nblocks)]
    got = [
        tuple(lax.ppermute(x, ("grp", "blk"), swap) for x in pair)
        for pair in (own_pair, from_m2, from_p2, far)
    ]
    pairs = [own_pair, from_m2, from_p2, from_m4, from_p4] + got
    key_blocks = jnp.stack([
        block_here, block_here - 2, block_here + 2, block_here - 4, block_here + 4,
        partner, partner - 2, partner + 2, partner - 4 + 8 * parity,
    ]).astype(jnp.int32)
    key_pos = (key_blocks[:, None] * frames + offsets[None, :]).reshape(-1)
    key_inside = ((key_blocks >= 0) & (key_blocks < nblocks))[:, None]
    key_rec = jnp.where(key_inside, segment_of(key_pos, starts).reshape(NBLK, frames), -1)
    rows = -(-NBLK // 8) * 8
    key_rec = jnp.pad(key_rec, ((0, rows - NBLK), (0, 0)), constant_values=-1)
    keys = [p[0] for p in pairs]
    vals = keys
    attended = attend(own_rec[:, None], key_rec, queries, keys, vals)
    projected = jnp.dot(attended, output_weight, preferred_element_type=jnp.float32)
    resid = lax.optimization_barrier(
        (features.astype(jnp.float32) + projected).astype(jnp.bfloat16)
    )
    resid32 = resid.astype(jnp.float32)
    center = jnp.mean(resid32, axis=1, keepdims=True)
    spread = jnp.mean((resid32 - center) ** 2, axis=1, keepdims=True)
    normed = ((resid32 - center) * lax.rsqrt(spread + 1e-05) * norm_gain + norm_bias).astype(
        jnp.bfloat16
    )
    rim_width = (depthwise_taps.shape[0] - 1) // 2
    head_rows = normed[:rim_width]
    tail_rows = normed[frames - rim_width :]
    cross = [(i, i + 1) for i in range(1, nblocks - 1, 2)]
    cross = cross + [(j, i) for i, j in cross]
    over_link = lax.ppermute(
        lax.select(parity == 0, head_rows, tail_rows), ("grp", "blk"), cross
    )
    on_chip = lax.ppermute(
        lax.select(parity == 0, tail_rows, head_rows), ("grp", "blk"), swap
    )
    low = lax.select(parity == 0, over_link, on_chip)
    high = lax.select(parity == 0, on_chip, over_link)
    extended = jnp.concatenate([low, normed, high], axis=0)
    ext_positions = (
        block_here * frames - rim_width + jnp.arange(frames + 2 * rim_width, dtype=jnp.int32)
    )
    ext_inside = (ext_positions >= 0) & (ext_positions < nblocks * frames)
    ext_rec = jnp.where(ext_inside, segment_of(ext_positions, starts), -1)
    extended32 = lax.optimization_barrier(extended).astype(jnp.float32)
    summed = jnp.zeros((frames, normed.shape[1]), jnp.float32)
    for tap in range(depthwise_taps.shape[0]):
        same_rec = (ext_rec[tap : tap + frames] == own_rec)[:, None]
        summed = summed + jnp.where(
            same_rec, extended32[tap : tap + frames] * depthwise_taps[tap], 0.0
        )
    shifted = summed * conv_gain + conv_bias
    act = lax.optimization_barrier((shifted * jax.nn.sigmoid(shifted)).astype(jnp.bfloat16))
    return (resid32 + jnp.dot(act, pointwise_weight, preferred_element_type=jnp.float32)).astype(
        jnp.bfloat16
    )


def solution(mesh):
    in_specs = (
        P(("grp", "blk"), None),
        P(("grp", "blk"), None),
        P(("grp", "blk"), None),
        P(("grp", "blk"), None),
        P(),
        P(),
        P(),
        P(),
        P(),
        P(),
        P(),
        P(),
    )
    out_specs = P(("grp", "blk"), None)
    return jax.shard_map(shards, mesh=mesh, in_specs=in_specs, out_specs=out_specs, check_vma=False)
```

```python
import jax
import jax.numpy as jnp
from jax import lax
from jax.sharding import PartitionSpec as P
from jax.experimental import pallas as pl
from jax.experimental.pallas import tpu as pltpu

HEADS = 12
HD = 64
REACH = 4


def shifted_2(block, axis, distance):
    devices = range(lax.axis_size(axis))
    route = [(i - distance, i) for i in devices if i - distance in devices]
    return lax.ppermute(block, axis, route)


def padded(block, sides, width):
    for axis, dim in sides:
        count = lax.axis_size(axis)
        forward = [(i, i + 1) for i in range(count - 1)]
        backward = [(target, source) for source, target in forward]
        low = lax.ppermute(
            lax.slice_in_dim(block, block.shape[dim] - width, None, axis=dim), axis, forward
        )
        high = lax.ppermute(lax.slice_in_dim(block, 0, width, axis=dim), axis, backward)
        block = jnp.concatenate([low, block, high], axis=dim)
    return block


def segment_of(positions, starts):
    return jnp.sum((starts[None, :] <= positions[:, None]).astype(jnp.int32), axis=1) - 1


def from_before(moving):
    return shifted_2(moving, ("grp", "blk"), 1)


def from_after(moving):
    return shifted_2(moving, ("grp", "blk"), -1)


NBLK = 2 * REACH + 1


def fold_lanes(x, op):
    width = x.shape[1]
    out = x[:, :128]
    for c in range(128, width, 128):
        out = op(out, x[:, c : c + 128])
    return out


def attend_kernel(recq_ref, reck_ref, q_ref, *refs):
    k_refs = refs[:NBLK]
    v_refs = refs[NBLK : 2 * NBLK]
    out_ref = refs[2 * NBLK]
    s_scr, bias_scr = refs[2 * NBLK + 1 :]

    @pl.when(pl.program_id(0) == 0)
    def _():
        rec_q = recq_ref[...]
        for j in range(NBLK):
            bias_scr[j] = jnp.where(rec_q == reck_ref[j : j + 1, :], 0.0, -1e30)

    for hh in range(q_ref.shape[1] // HD):
        cols = slice(hh * HD, (hh + 1) * HD)
        q_h = (q_ref[:, cols].astype(jnp.float32) * (HD ** (-0.5))).astype(q_ref.dtype)
        wide_top = None
        for j in range(NBLK):
            s = lax.dot_general(
                q_h, k_refs[j][:, cols], (((1,), (1,)), ((), ())),
                preferred_element_type=jnp.float32,
            ) + bias_scr[j]
            s_scr[j] = s
            part = fold_lanes(s, jnp.maximum)
            wide_top = part if wide_top is None else jnp.maximum(wide_top, part)
        top = jnp.max(wide_top, axis=1, keepdims=True)
        wide_total = None
        acc = None
        for j in range(NBLK):
            p = jnp.exp(s_scr[j] - top)
            part = fold_lanes(p, jnp.add)
            prod = jnp.dot(p.astype(jnp.bfloat16), v_refs[j][:, cols],
                           preferred_element_type=jnp.float32)
            wide_total = part if wide_total is None else wide_total + part
            acc = prod if acc is None else acc + prod
        total = jnp.sum(wide_total, axis=1, keepdims=True)
        out_ref[:, cols] = (acc / total).astype(out_ref.dtype)


def attend(rec_q, rec_k, query, keys, vals):
    frames, width = query.shape
    pair = 4 * HD
    tile = pl.BlockSpec((frames, pair), lambda g: (0, g))
    v_tile = pl.BlockSpec((frames, pair), lambda g: (1, g))
    return pl.pallas_call(
        attend_kernel,
        grid=(width // pair,),
        in_specs=[
            pl.BlockSpec(rec_q.shape, lambda g: (0, 0)),
            pl.BlockSpec(rec_k.shape, lambda g: (0, 0)),
            tile,
        ]
        + [tile] * NBLK
        + [v_tile] * NBLK,
        out_specs=tile,
        out_shape=jax.ShapeDtypeStruct((frames, width), jnp.bfloat16),
        scratch_shapes=[pltpu.VMEM((NBLK, frames, frames), jnp.float32)] * 2,
    )(rec_q, rec_k, query, *keys, *vals)


def shards(
    features,
    queries,
    key_vectors,
    values,
    record_lengths,
    output_weight,
    norm_gain,
    norm_bias,
    depthwise_taps,
    conv_gain,
    conv_bias,
    pointwise_weight,
):
    frames = features.shape[0]
    per_group = lax.axis_size("blk")
    nblocks = lax.axis_size("grp") * per_group
    block_here = lax.axis_index("grp") * per_group + lax.axis_index("blk")
    rec_ends = jnp.cumsum(record_lengths)
    starts = rec_ends - record_lengths
    offsets = jnp.arange(frames, dtype=jnp.int32)
    own_rec = segment_of(block_here * frames + offsets, starts)

    def hop(pair, distance):
        return tuple(shifted_2(x, ("grp", "blk"), distance) for x in pair)

    own_pair = (jnp.concatenate([key_vectors, values], axis=0),)
    from_m2 = hop(own_pair, 2)
    from_p2 = hop(own_pair, -2)
    from_m4 = hop(from_m2, 2)
    from_p4 = hop(from_p2, -2)
    parity = block_here % 2
    partner = block_here + 1 - 2 * parity
    far = tuple(lax.select(parity == 0, p4, m4) for m4, p4 in zip(from_m4, from_p4))
    swap = [(i, i ^ 1) for i in range(nblocks)]
    got = [
        tuple(lax.ppermute(x, ("grp", "blk"), swap) for x in pair)
        for pair in (own_pair, from_m2, from_p2, far)
    ]
    pairs = [own_pair, from_m2, from_p2, from_m4, from_p4] + got
    key_blocks = jnp.stack([
        block_here, block_here - 2, block_here + 2, block_here - 4, block_here + 4,
        partner, partner - 2, partner + 2, partner - 4 + 8 * parity,
    ]).astype(jnp.int32)
    key_pos = (key_blocks[:, None] * frames + offsets[None, :]).reshape(-1)
    key_inside = ((key_blocks >= 0) & (key_blocks < nblocks))[:, None]
    key_rec = jnp.where(key_inside, segment_of(key_pos, starts).reshape(NBLK, frames), -1)
    rows = -(-NBLK // 8) * 8
    key_rec = jnp.pad(key_rec, ((0, rows - NBLK), (0, 0)), constant_values=-1)
    keys = [p[0] for p in pairs]
    vals = keys
    attended = attend(own_rec[:, None], key_rec, queries, keys, vals)
    projected = jnp.dot(attended, output_weight, preferred_element_type=jnp.float32)
    resid = lax.optimization_barrier(
        (features.astype(jnp.float32) + projected).astype(jnp.bfloat16)
    )
    resid32 = resid.astype(jnp.float32)
    center = jnp.mean(resid32, axis=1, keepdims=True)
    spread = jnp.mean((resid32 - center) ** 2, axis=1, keepdims=True)
    normed = ((resid32 - center) * lax.rsqrt(spread + 1e-05) * norm_gain + norm_bias).astype(
        jnp.bfloat16
    )
    rim_width = (depthwise_taps.shape[0] - 1) // 2
    head_rows = normed[:rim_width]
    tail_rows = normed[frames - rim_width :]
    cross = [(i, i + 1) for i in range(1, nblocks - 1, 2)]
    cross = cross + [(j, i) for i, j in cross]
    over_link = lax.ppermute(
        lax.select(parity == 0, head_rows, tail_rows), ("grp", "blk"), cross
    )
    on_chip = lax.ppermute(
        lax.select(parity == 0, tail_rows, head_rows), ("grp", "blk"), swap
    )
    low = lax.select(parity == 0, over_link, on_chip)
    high = lax.select(parity == 0, on_chip, over_link)
    extended = jnp.concatenate([low, normed, high], axis=0)
    ext_positions = (
        block_here * frames - rim_width + jnp.arange(frames + 2 * rim_width, dtype=jnp.int32)
    )
    ext_inside = (ext_positions >= 0) & (ext_positions < nblocks * frames)
    ext_rec = jnp.where(ext_inside, segment_of(ext_positions, starts), -1)
    extended32 = lax.optimization_barrier(extended).astype(jnp.float32)
    summed = jnp.zeros((frames, normed.shape[1]), jnp.float32)
    for tap in range(depthwise_taps.shape[0]):
        same_rec = (ext_rec[tap : tap + frames] == own_rec)[:, None]
        summed = summed + jnp.where(
            same_rec, extended32[tap : tap + frames] * depthwise_taps[tap], 0.0
        )
    shifted = summed * conv_gain + conv_bias
    act = lax.optimization_barrier((shifted * jax.nn.sigmoid(shifted)).astype(jnp.bfloat16))
    return (resid32 + jnp.dot(act, pointwise_weight, preferred_element_type=jnp.float32)).astype(
        jnp.bfloat16
    )


def solution(mesh):
    in_specs = (
        P(("grp", "blk"), None),
        P(("grp", "blk"), None),
        P(("grp", "blk"), None),
        P(("grp", "blk"), None),
        P(),
        P(),
        P(),
        P(),
        P(),
        P(),
        P(),
        P(),
    )
    out_specs = P(("grp", "blk"), None)
    return jax.shard_map(shards, mesh=mesh, in_specs=in_specs, out_specs=out_specs, check_vma=False)
```

```python
import jax
import jax.numpy as jnp
from jax import lax
from jax.sharding import PartitionSpec as P
from jax.experimental import pallas as pl
from jax.experimental.pallas import tpu as pltpu

HEADS = 12
HD = 64
REACH = 4


def shifted_2(block, axis, distance):
    devices = range(lax.axis_size(axis))
    route = [(i - distance, i) for i in devices if i - distance in devices]
    return lax.ppermute(block, axis, route)


def padded(block, sides, width):
    for axis, dim in sides:
        count = lax.axis_size(axis)
        forward = [(i, i + 1) for i in range(count - 1)]
        backward = [(target, source) for source, target in forward]
        low = lax.ppermute(
            lax.slice_in_dim(block, block.shape[dim] - width, None, axis=dim), axis, forward
        )
        high = lax.ppermute(lax.slice_in_dim(block, 0, width, axis=dim), axis, backward)
        block = jnp.concatenate([low, block, high], axis=dim)
    return block


def segment_of(positions, starts):
    return jnp.sum((starts[None, :] <= positions[:, None]).astype(jnp.int32), axis=1) - 1


def from_before(moving):
    return shifted_2(moving, ("grp", "blk"), 1)


def from_after(moving):
    return shifted_2(moving, ("grp", "blk"), -1)


NBLK = 2 * REACH + 1


def fold_lanes(x, op):
    width = x.shape[1]
    out = x[:, :128]
    for c in range(128, width, 128):
        out = op(out, x[:, c : c + 128])
    return out


def attend_kernel(recq_ref, reck_ref, q_ref, *refs):
    k_refs = refs[:NBLK]
    v_refs = refs[NBLK : 2 * NBLK]
    out_ref = refs[2 * NBLK]
    s_scr, bias_scr = refs[2 * NBLK + 1 :]

    @pl.when(pl.program_id(0) == 0)
    def _():
        rec_q = recq_ref[...]
        for j in range(NBLK):
            bias_scr[j] = jnp.where(rec_q == reck_ref[j : j + 1, :], 0.0, -1e30)

    for hh in range(q_ref.shape[1] // HD):
        cols = slice(hh * HD, (hh + 1) * HD)
        q_h = (q_ref[:, cols].astype(jnp.float32) * (HD ** (-0.5))).astype(q_ref.dtype)
        wide_top = None
        for j in range(NBLK):
            s = lax.dot_general(
                q_h, k_refs[j][:, cols], (((1,), (1,)), ((), ())),
                preferred_element_type=jnp.float32,
            ) + bias_scr[j]
            s_scr[j] = s
            part = fold_lanes(s, jnp.maximum)
            wide_top = part if wide_top is None else jnp.maximum(wide_top, part)
        top = jnp.max(wide_top, axis=1, keepdims=True)
        wide_total = None
        acc = None
        for j in range(NBLK):
            p = jnp.exp(s_scr[j] - top)
            part = fold_lanes(p, jnp.add)
            prod = jnp.dot(p.astype(jnp.bfloat16), v_refs[j][:, cols],
                           preferred_element_type=jnp.float32)
            wide_total = part if wide_total is None else wide_total + part
            acc = prod if acc is None else acc + prod
        total = jnp.sum(wide_total, axis=1, keepdims=True)
        out_ref[:, cols] = (acc / total).astype(out_ref.dtype)


def attend(rec_q, rec_k, query, keys, vals):
    frames, width = query.shape
    pair = 4 * HD
    tile = pl.BlockSpec((frames, pair), lambda g: (0, g))
    v_tile = pl.BlockSpec((frames, pair), lambda g: (1, g))
    return pl.pallas_call(
        attend_kernel,
        grid=(width // pair,),
        in_specs=[
            pl.BlockSpec(rec_q.shape, lambda g: (0, 0)),
            pl.BlockSpec(rec_k.shape, lambda g: (0, 0)),
            tile,
        ]
        + [tile] * NBLK
        + [v_tile] * NBLK,
        out_specs=tile,
        out_shape=jax.ShapeDtypeStruct((frames, width), jnp.bfloat16),
        scratch_shapes=[pltpu.VMEM((NBLK, frames, frames), jnp.float32)] * 2,
    )(rec_q, rec_k, query, *keys, *vals)


def stack_kernel(k_hbm, v_hbm, out_hbm, sems):
    rows = k_hbm.shape[0]
    first = pltpu.make_async_copy(k_hbm, out_hbm.at[pl.ds(0, rows)], sems.at[0])
    second = pltpu.make_async_copy(v_hbm, out_hbm.at[pl.ds(rows, rows)], sems.at[1])
    first.start()
    second.start()
    first.wait()
    second.wait()


def stack_rows(top, bottom):
    rows, width = top.shape
    return pl.pallas_call(
        stack_kernel,
        in_specs=[pl.BlockSpec(memory_space=pl.ANY)] * 2,
        out_specs=pl.BlockSpec(memory_space=pl.ANY),
        out_shape=jax.ShapeDtypeStruct((2 * rows, width), top.dtype),
        scratch_shapes=[pltpu.SemaphoreType.DMA((2,))],
    )(top, bottom)


def shards(
    features,
    queries,
    key_vectors,
    values,
    record_lengths,
    output_weight,
    norm_gain,
    norm_bias,
    depthwise_taps,
    conv_gain,
    conv_bias,
    pointwise_weight,
):
    frames = features.shape[0]
    per_group = lax.axis_size("blk")
    nblocks = lax.axis_size("grp") * per_group
    block_here = lax.axis_index("grp") * per_group + lax.axis_index("blk")
    rec_ends = jnp.cumsum(record_lengths)
    starts = rec_ends - record_lengths
    offsets = jnp.arange(frames, dtype=jnp.int32)
    own_rec = segment_of(block_here * frames + offsets, starts)

    def hop(pair, distance):
        return tuple(shifted_2(x, ("grp", "blk"), distance) for x in pair)

    own_pair = (stack_rows(key_vectors, values),)
    from_m2 = hop(own_pair, 2)
    from_p2 = hop(own_pair, -2)
    from_m4 = hop(from_m2, 2)
    from_p4 = hop(from_p2, -2)
    parity = block_here % 2
    partner = block_here + 1 - 2 * parity
    far = tuple(lax.select(parity == 0, p4, m4) for m4, p4 in zip(from_m4, from_p4))
    swap = [(i, i ^ 1) for i in range(nblocks)]
    got = [
        tuple(lax.ppermute(x, ("grp", "blk"), swap) for x in pair)
        for pair in (own_pair, from_m2, from_p2, far)
    ]
    pairs = [own_pair, from_m2, from_p2, from_m4, from_p4] + got
    key_blocks = jnp.stack([
        block_here, block_here - 2, block_here + 2, block_here - 4, block_here + 4,
        partner, partner - 2, partner + 2, partner - 4 + 8 * parity,
    ]).astype(jnp.int32)
    key_pos = (key_blocks[:, None] * frames + offsets[None, :]).reshape(-1)
    key_inside = ((key_blocks >= 0) & (key_blocks < nblocks))[:, None]
    key_rec = jnp.where(key_inside, segment_of(key_pos, starts).reshape(NBLK, frames), -1)
    rows = -(-NBLK // 8) * 8
    key_rec = jnp.pad(key_rec, ((0, rows - NBLK), (0, 0)), constant_values=-1)
    keys = [p[0] for p in pairs]
    vals = keys
    attended = attend(own_rec[:, None], key_rec, queries, keys, vals)
    projected = jnp.dot(attended, output_weight, preferred_element_type=jnp.float32)
    resid = lax.optimization_barrier(
        (features.astype(jnp.float32) + projected).astype(jnp.bfloat16)
    )
    resid32 = resid.astype(jnp.float32)
    center = jnp.mean(resid32, axis=1, keepdims=True)
    spread = jnp.mean((resid32 - center) ** 2, axis=1, keepdims=True)
    normed = ((resid32 - center) * lax.rsqrt(spread + 1e-05) * norm_gain + norm_bias).astype(
        jnp.bfloat16
    )
    rim_width = (depthwise_taps.shape[0] - 1) // 2
    head_rows = normed[:rim_width]
    tail_rows = normed[frames - rim_width :]
    cross = [(i, i + 1) for i in range(1, nblocks - 1, 2)]
    cross = cross + [(j, i) for i, j in cross]
    over_link = lax.ppermute(
        lax.select(parity == 0, head_rows, tail_rows), ("grp", "blk"), cross
    )
    on_chip = lax.ppermute(
        lax.select(parity == 0, tail_rows, head_rows), ("grp", "blk"), swap
    )
    low = lax.select(parity == 0, over_link, on_chip)
    high = lax.select(parity == 0, on_chip, over_link)
    extended = jnp.concatenate([low, normed, high], axis=0)
    ext_positions = (
        block_here * frames - rim_width + jnp.arange(frames + 2 * rim_width, dtype=jnp.int32)
    )
    ext_inside = (ext_positions >= 0) & (ext_positions < nblocks * frames)
    ext_rec = jnp.where(ext_inside, segment_of(ext_positions, starts), -1)
    extended32 = lax.optimization_barrier(extended).astype(jnp.float32)
    summed = jnp.zeros((frames, normed.shape[1]), jnp.float32)
    for tap in range(depthwise_taps.shape[0]):
        same_rec = (ext_rec[tap : tap + frames] == own_rec)[:, None]
        summed = summed + jnp.where(
            same_rec, extended32[tap : tap + frames] * depthwise_taps[tap], 0.0
        )
    shifted = summed * conv_gain + conv_bias
    act = lax.optimization_barrier((shifted * jax.nn.sigmoid(shifted)).astype(jnp.bfloat16))
    return (resid32 + jnp.dot(act, pointwise_weight, preferred_element_type=jnp.float32)).astype(
        jnp.bfloat16
    )


def solution(mesh):
    in_specs = (
        P(("grp", "blk"), None),
        P(("grp", "blk"), None),
        P(("grp", "blk"), None),
        P(("grp", "blk"), None),
        P(),
        P(),
        P(),
        P(),
        P(),
        P(),
        P(),
        P(),
    )
    out_specs = P(("grp", "blk"), None)
    return jax.shard_map(shards, mesh=mesh, in_specs=in_specs, out_specs=out_specs, check_vma=False)
```

```python
import jax
import jax.numpy as jnp
from jax import lax
from jax.sharding import PartitionSpec as P
from jax.experimental import pallas as pl
from jax.experimental.pallas import tpu as pltpu

HEADS = 12
HD = 64
REACH = 4


def shifted_2(block, axis, distance):
    devices = range(lax.axis_size(axis))
    route = [(i - distance, i) for i in devices if i - distance in devices]
    return lax.ppermute(block, axis, route)


def padded(block, sides, width):
    for axis, dim in sides:
        count = lax.axis_size(axis)
        forward = [(i, i + 1) for i in range(count - 1)]
        backward = [(target, source) for source, target in forward]
        low = lax.ppermute(
            lax.slice_in_dim(block, block.shape[dim] - width, None, axis=dim), axis, forward
        )
        high = lax.ppermute(lax.slice_in_dim(block, 0, width, axis=dim), axis, backward)
        block = jnp.concatenate([low, block, high], axis=dim)
    return block


def segment_of(positions, starts):
    return jnp.sum((starts[None, :] <= positions[:, None]).astype(jnp.int32), axis=1) - 1


def from_before(moving):
    return shifted_2(moving, ("grp", "blk"), 1)


def from_after(moving):
    return shifted_2(moving, ("grp", "blk"), -1)


NBLK = 2 * REACH + 1


def fold_lanes(x, op):
    width = x.shape[1]
    out = x[:, :128]
    for c in range(128, width, 128):
        out = op(out, x[:, c : c + 128])
    return out


def attend_kernel(recq_ref, reck_ref, q_ref, w_ref, feat_ref, *refs):
    k_refs = refs[:NBLK]
    v_refs = refs[NBLK : 2 * NBLK]
    resid_ref = refs[2 * NBLK]
    s_scr, bias_scr, att_scr, proj_scr = refs[2 * NBLK + 1 :]

    @pl.when(pl.program_id(0) == 0)
    def _():
        rec_q = recq_ref[...]
        for j in range(NBLK):
            bias_scr[j] = jnp.where(rec_q == reck_ref[j : j + 1, :], 0.0, -1e30)

    for hh in range(q_ref.shape[1] // HD):
        cols = slice(hh * HD, (hh + 1) * HD)
        q_h = (q_ref[:, cols].astype(jnp.float32) * (HD ** (-0.5))).astype(q_ref.dtype)
        wide_top = None
        for j in range(NBLK):
            s = lax.dot_general(
                q_h, k_refs[j][:, cols], (((1,), (1,)), ((), ())),
                preferred_element_type=jnp.float32,
            ) + bias_scr[j]
            s_scr[j] = s
            part = fold_lanes(s, jnp.maximum)
            wide_top = part if wide_top is None else jnp.maximum(wide_top, part)
        top = jnp.max(wide_top, axis=1, keepdims=True)
        wide_total = None
        acc = None
        for j in range(NBLK):
            p = jnp.exp(s_scr[j] - top)
            part = fold_lanes(p, jnp.add)
            prod = jnp.dot(p.astype(jnp.bfloat16), v_refs[j][:, cols],
                           preferred_element_type=jnp.float32)
            wide_total = part if wide_total is None else wide_total + part
            acc = prod if acc is None else acc + prod
        total = jnp.sum(wide_total, axis=1, keepdims=True)
        att_scr[:, cols] = (acc / total).astype(att_scr.dtype)

    step = pl.program_id(0)
    prod = jnp.dot(att_scr[...], w_ref[...], preferred_element_type=jnp.float32)

    @pl.when(step == 0)
    def _():
        proj_scr[...] = prod

    @pl.when(step > 0)
    def _():
        proj_scr[...] += prod

    @pl.when(step == pl.num_programs(0) - 1)
    def _():
        resid_ref[...] = (feat_ref[...].astype(jnp.float32) + proj_scr[...]).astype(resid_ref.dtype)


def attend(rec_q, rec_k, query, keys, vals, out_w, features):
    frames, width = query.shape
    pair = 4 * HD
    tile = pl.BlockSpec((frames, pair), lambda g: (0, g))
    v_tile = pl.BlockSpec((frames, pair), lambda g: (1, g))
    whole = pl.BlockSpec(features.shape, lambda g: (0, 0))
    return pl.pallas_call(
        attend_kernel,
        grid=(width // pair,),
        in_specs=[
            pl.BlockSpec(rec_q.shape, lambda g: (0, 0)),
            pl.BlockSpec(rec_k.shape, lambda g: (0, 0)),
            tile,
            pl.BlockSpec((pair, out_w.shape[1]), lambda g: (g, 0)),
            whole,
        ]
        + [tile] * NBLK
        + [v_tile] * NBLK,
        out_specs=whole,
        out_shape=jax.ShapeDtypeStruct(features.shape, jnp.bfloat16),
        scratch_shapes=[pltpu.VMEM((NBLK, frames, frames), jnp.float32)] * 2
        + [pltpu.VMEM((frames, pair), jnp.bfloat16), pltpu.VMEM(features.shape, jnp.float32)],
    )(rec_q, rec_k, query, out_w, features, *keys, *vals)


def shards(
    features,
    queries,
    key_vectors,
    values,
    record_lengths,
    output_weight,
    norm_gain,
    norm_bias,
    depthwise_taps,
    conv_gain,
    conv_bias,
    pointwise_weight,
):
    frames = features.shape[0]
    per_group = lax.axis_size("blk")
    nblocks = lax.axis_size("grp") * per_group
    block_here = lax.axis_index("grp") * per_group + lax.axis_index("blk")
    rec_ends = jnp.cumsum(record_lengths)
    starts = rec_ends - record_lengths
    offsets = jnp.arange(frames, dtype=jnp.int32)
    own_rec = segment_of(block_here * frames + offsets, starts)

    def hop(pair, distance):
        return tuple(shifted_2(x, ("grp", "blk"), distance) for x in pair)

    own_pair = (jnp.concatenate([key_vectors, values], axis=0),)
    from_m2 = hop(own_pair, 2)
    from_p2 = hop(own_pair, -2)
    from_m4 = hop(from_m2, 2)
    from_p4 = hop(from_p2, -2)
    parity = block_here % 2
    partner = block_here + 1 - 2 * parity
    far = tuple(lax.select(parity == 0, p4, m4) for m4, p4 in zip(from_m4, from_p4))
    swap = [(i, i ^ 1) for i in range(nblocks)]
    got = [
        tuple(lax.ppermute(x, ("grp", "blk"), swap) for x in pair)
        for pair in (own_pair, from_m2, from_p2, far)
    ]
    pairs = [own_pair, from_m2, from_p2, from_m4, from_p4] + got
    key_blocks = jnp.stack([
        block_here, block_here - 2, block_here + 2, block_here - 4, block_here + 4,
        partner, partner - 2, partner + 2, partner - 4 + 8 * parity,
    ]).astype(jnp.int32)
    key_pos = (key_blocks[:, None] * frames + offsets[None, :]).reshape(-1)
    key_inside = ((key_blocks >= 0) & (key_blocks < nblocks))[:, None]
    key_rec = jnp.where(key_inside, segment_of(key_pos, starts).reshape(NBLK, frames), -1)
    rows = -(-NBLK // 8) * 8
    key_rec = jnp.pad(key_rec, ((0, rows - NBLK), (0, 0)), constant_values=-1)
    keys = [p[0] for p in pairs]
    vals = keys
    resid = lax.optimization_barrier(
        attend(own_rec[:, None], key_rec, queries, keys, vals, output_weight, features)
    )
    resid32 = resid.astype(jnp.float32)
    center = jnp.mean(resid32, axis=1, keepdims=True)
    spread = jnp.mean((resid32 - center) ** 2, axis=1, keepdims=True)
    normed = ((resid32 - center) * lax.rsqrt(spread + 1e-05) * norm_gain + norm_bias).astype(
        jnp.bfloat16
    )
    rim_width = (depthwise_taps.shape[0] - 1) // 2
    head_rows = normed[:rim_width]
    tail_rows = normed[frames - rim_width :]
    cross = [(i, i + 1) for i in range(1, nblocks - 1, 2)]
    cross = cross + [(j, i) for i, j in cross]
    over_link = lax.ppermute(
        lax.select(parity == 0, head_rows, tail_rows), ("grp", "blk"), cross
    )
    on_chip = lax.ppermute(
        lax.select(parity == 0, tail_rows, head_rows), ("grp", "blk"), swap
    )
    low = lax.select(parity == 0, over_link, on_chip)
    high = lax.select(parity == 0, on_chip, over_link)
    extended = jnp.concatenate([low, normed, high], axis=0)
    ext_positions = (
        block_here * frames - rim_width + jnp.arange(frames + 2 * rim_width, dtype=jnp.int32)
    )
    ext_inside = (ext_positions >= 0) & (ext_positions < nblocks * frames)
    ext_rec = jnp.where(ext_inside, segment_of(ext_positions, starts), -1)
    extended32 = lax.optimization_barrier(extended).astype(jnp.float32)
    summed = jnp.zeros((frames, normed.shape[1]), jnp.float32)
    for tap in range(depthwise_taps.shape[0]):
        same_rec = (ext_rec[tap : tap + frames] == own_rec)[:, None]
        summed = summed + jnp.where(
            same_rec, extended32[tap : tap + frames] * depthwise_taps[tap], 0.0
        )
    shifted = summed * conv_gain + conv_bias
    act = lax.optimization_barrier((shifted * jax.nn.sigmoid(shifted)).astype(jnp.bfloat16))
    return (resid32 + jnp.dot(act, pointwise_weight, preferred_element_type=jnp.float32)).astype(
        jnp.bfloat16
    )


def solution(mesh):
    in_specs = (
        P(("grp", "blk"), None),
        P(("grp", "blk"), None),
        P(("grp", "blk"), None),
        P(("grp", "blk"), None),
        P(),
        P(),
        P(),
        P(),
        P(),
        P(),
        P(),
        P(),
    )
    out_specs = P(("grp", "blk"), None)
    return jax.shard_map(shards, mesh=mesh, in_specs=in_specs, out_specs=out_specs, check_vma=False)
```

```python
import jax
import jax.numpy as jnp
from jax import lax
from jax.sharding import PartitionSpec as P
from jax.experimental import pallas as pl
from jax.experimental.pallas import tpu as pltpu

HEADS = 12
HD = 64
REACH = 4


def shifted_2(block, axis, distance):
    devices = range(lax.axis_size(axis))
    route = [(i - distance, i) for i in devices if i - distance in devices]
    return lax.ppermute(block, axis, route)


def padded(block, sides, width):
    for axis, dim in sides:
        count = lax.axis_size(axis)
        forward = [(i, i + 1) for i in range(count - 1)]
        backward = [(target, source) for source, target in forward]
        low = lax.ppermute(
            lax.slice_in_dim(block, block.shape[dim] - width, None, axis=dim), axis, forward
        )
        high = lax.ppermute(lax.slice_in_dim(block, 0, width, axis=dim), axis, backward)
        block = jnp.concatenate([low, block, high], axis=dim)
    return block


def segment_of(positions, starts):
    return jnp.sum((starts[None, :] <= positions[:, None]).astype(jnp.int32), axis=1) - 1


def from_before(moving):
    return shifted_2(moving, ("grp", "blk"), 1)


def from_after(moving):
    return shifted_2(moving, ("grp", "blk"), -1)


NBLK = 2 * REACH + 1


def fold_lanes(x, op):
    width = x.shape[1]
    out = x[:, :128]
    for c in range(128, width, 128):
        out = op(out, x[:, c : c + 128])
    return out


def attend_kernel(recq_ref, reck_ref, q_ref, *refs):
    k_refs = refs[:NBLK]
    v_refs = refs[NBLK : 2 * NBLK]
    out_ref = refs[2 * NBLK]
    s_scr, bias_scr = refs[2 * NBLK + 1 :]

    @pl.when(pl.program_id(0) == 0)
    def _():
        rec_q = recq_ref[...]
        for j in range(NBLK):
            bias_scr[j] = jnp.where(rec_q == reck_ref[j : j + 1, :], 0.0, -1e30)

    for hh in range(q_ref.shape[1] // HD):
        cols = slice(hh * HD, (hh + 1) * HD)
        q_h = (q_ref[:, cols].astype(jnp.float32) * (HD ** (-0.5))).astype(q_ref.dtype)
        wide_top = None
        for j in range(NBLK):
            s = lax.dot_general(
                q_h, k_refs[j][:, cols], (((1,), (1,)), ((), ())),
                preferred_element_type=jnp.float32,
            ) + bias_scr[j]
            s_scr[j] = s
            part = fold_lanes(s, jnp.maximum)
            wide_top = part if wide_top is None else jnp.maximum(wide_top, part)
        top = jnp.max(wide_top, axis=1, keepdims=True)
        wide_total = None
        acc = None
        for j in range(NBLK):
            p = jnp.exp(s_scr[j] - top)
            part = fold_lanes(p, jnp.add)
            prod = jnp.dot(p.astype(jnp.bfloat16), v_refs[j][:, cols],
                           preferred_element_type=jnp.float32)
            wide_total = part if wide_total is None else wide_total + part
            acc = prod if acc is None else acc + prod
        total = jnp.sum(wide_total, axis=1, keepdims=True)
        out_ref[:, cols] = (acc / total).astype(out_ref.dtype)


def attend(rec_q, rec_k, query, keys, vals):
    frames, width = query.shape
    pair = 4 * HD
    tile = pl.BlockSpec((frames, pair), lambda g: (0, g))
    v_tile = pl.BlockSpec((frames, pair), lambda g: (1, g))
    return pl.pallas_call(
        attend_kernel,
        grid=(width // pair,),
        in_specs=[
            pl.BlockSpec(rec_q.shape, lambda g: (0, 0)),
            pl.BlockSpec(rec_k.shape, lambda g: (0, 0)),
            tile,
        ]
        + [tile] * NBLK
        + [v_tile] * NBLK,
        out_specs=tile,
        out_shape=jax.ShapeDtypeStruct((frames, width), jnp.bfloat16),
        scratch_shapes=[pltpu.VMEM((NBLK, frames, frames), jnp.float32)] * 2,
    )(rec_q, rec_k, query, *keys, *vals)


def shards(
    features,
    queries,
    key_vectors,
    values,
    record_lengths,
    output_weight,
    norm_gain,
    norm_bias,
    depthwise_taps,
    conv_gain,
    conv_bias,
    pointwise_weight,
):
    frames = features.shape[0]
    per_group = lax.axis_size("blk")
    nblocks = lax.axis_size("grp") * per_group
    block_here = lax.axis_index("grp") * per_group + lax.axis_index("blk")
    rec_ends = jnp.cumsum(record_lengths)
    starts = rec_ends - record_lengths
    offsets = jnp.arange(frames, dtype=jnp.int32)
    own_rec = segment_of(block_here * frames + offsets, starts)

    def hop(pair, distance):
        return tuple(shifted_2(x, ("grp", "blk"), distance) for x in pair)

    stacked_rows = lax.broadcasted_iota(jnp.int32, (2 * frames, 1), 0)
    own_pair = (
        jnp.where(
            stacked_rows < frames,
            jnp.pad(key_vectors, ((0, frames), (0, 0))),
            jnp.pad(values, ((frames, 0), (0, 0))),
        ),
    )
    from_m2 = hop(own_pair, 2)
    from_p2 = hop(own_pair, -2)
    from_m4 = hop(from_m2, 2)
    from_p4 = hop(from_p2, -2)
    parity = block_here % 2
    partner = block_here + 1 - 2 * parity
    far = tuple(lax.select(parity == 0, p4, m4) for m4, p4 in zip(from_m4, from_p4))
    swap = [(i, i ^ 1) for i in range(nblocks)]
    got = [
        tuple(lax.ppermute(x, ("grp", "blk"), swap) for x in pair)
        for pair in (own_pair, from_m2, from_p2, far)
    ]
    pairs = [own_pair, from_m2, from_p2, from_m4, from_p4] + got
    key_blocks = jnp.stack([
        block_here, block_here - 2, block_here + 2, block_here - 4, block_here + 4,
        partner, partner - 2, partner + 2, partner - 4 + 8 * parity,
    ]).astype(jnp.int32)
    key_pos = (key_blocks[:, None] * frames + offsets[None, :]).reshape(-1)
    key_inside = ((key_blocks >= 0) & (key_blocks < nblocks))[:, None]
    key_rec = jnp.where(key_inside, segment_of(key_pos, starts).reshape(NBLK, frames), -1)
    rows = -(-NBLK // 8) * 8
    key_rec = jnp.pad(key_rec, ((0, rows - NBLK), (0, 0)), constant_values=-1)
    keys = [p[0] for p in pairs]
    vals = keys
    attended = attend(own_rec[:, None], key_rec, queries, keys, vals)
    projected = jnp.dot(attended, output_weight, preferred_element_type=jnp.float32)
    resid = lax.optimization_barrier(
        (features.astype(jnp.float32) + projected).astype(jnp.bfloat16)
    )
    resid32 = resid.astype(jnp.float32)
    center = jnp.mean(resid32, axis=1, keepdims=True)
    spread = jnp.mean((resid32 - center) ** 2, axis=1, keepdims=True)
    normed = ((resid32 - center) * lax.rsqrt(spread + 1e-05) * norm_gain + norm_bias).astype(
        jnp.bfloat16
    )
    rim_width = (depthwise_taps.shape[0] - 1) // 2
    head_rows = normed[:rim_width]
    tail_rows = normed[frames - rim_width :]
    cross = [(i, i + 1) for i in range(1, nblocks - 1, 2)]
    cross = cross + [(j, i) for i, j in cross]
    over_link = lax.ppermute(
        lax.select(parity == 0, head_rows, tail_rows), ("grp", "blk"), cross
    )
    on_chip = lax.ppermute(
        lax.select(parity == 0, tail_rows, head_rows), ("grp", "blk"), swap
    )
    low = lax.select(parity == 0, over_link, on_chip)
    high = lax.select(parity == 0, on_chip, over_link)
    extended = jnp.concatenate([low, normed, high], axis=0)
    ext_positions = (
        block_here * frames - rim_width + jnp.arange(frames + 2 * rim_width, dtype=jnp.int32)
    )
    ext_inside = (ext_positions >= 0) & (ext_positions < nblocks * frames)
    ext_rec = jnp.where(ext_inside, segment_of(ext_positions, starts), -1)
    extended32 = lax.optimization_barrier(extended).astype(jnp.float32)
    summed = jnp.zeros((frames, normed.shape[1]), jnp.float32)
    for tap in range(depthwise_taps.shape[0]):
        same_rec = (ext_rec[tap : tap + frames] == own_rec)[:, None]
        summed = summed + jnp.where(
            same_rec, extended32[tap : tap + frames] * depthwise_taps[tap], 0.0
        )
    shifted = summed * conv_gain + conv_bias
    act = lax.optimization_barrier((shifted * jax.nn.sigmoid(shifted)).astype(jnp.bfloat16))
    return (resid32 + jnp.dot(act, pointwise_weight, preferred_element_type=jnp.float32)).astype(
        jnp.bfloat16
    )


def solution(mesh):
    in_specs = (
        P(("grp", "blk"), None),
        P(("grp", "blk"), None),
        P(("grp", "blk"), None),
        P(("grp", "blk"), None),
        P(),
        P(),
        P(),
        P(),
        P(),
        P(),
        P(),
        P(),
    )
    out_specs = P(("grp", "blk"), None)
    return jax.shard_map(shards, mesh=mesh, in_specs=in_specs, out_specs=out_specs, check_vma=False)
```
